256 devices in a mesh: expert: 64 (over y, z, core), tensor: 4 (over x).
Axes of the slice: x: 4, y: 4, z: 8, core: 2. Of those that a mesh axis runs over, the one named last changes fastest.
Arguments:
- tokens: bfloat16 [8192, 2048], P('expert', 'tensor'), may hold values from -6 to 6
- labels: int32 [8192, 1], P('expert'), may hold values from 0 to 31, as said below
- domain_ids: int32 [8192], P('expert'), may hold values from 0 to 21
- domain_weights: float32 [22], replicated, may hold values from 0.02 to 0.5
- cotangent: bfloat16 [8192, 2048], P('expert', 'tensor'), may hold values from -6 to 6
- gate_weight: bfloat16 [64, 2048, 2048], P('expert', None, 'tensor'), may hold values from -0.125 to 0.125
- up_weight: bfloat16 [64, 2048, 2048], P('expert', None, 'tensor'), may hold values from -0.125 to 0.125
- down_weight: bfloat16 [64, 2048, 2048], P('expert', 'tensor'), may hold values from -0.09375 to 0.09375
Outputs:
- layer_out: bfloat16 [8192, 2048], P('expert', 'tensor')
- input_grad: bfloat16 [8192, 2048], P('expert', 'tensor')
- gate_grad: bfloat16 [64, 2048, 2048], P('expert', None, 'tensor')
- up_grad: bfloat16 [64, 2048, 2048], P('expert', None, 'tensor')
- down_grad: bfloat16 [64, 2048, 2048], P('expert', 'tensor')
The draws below stay inside these ranges and needn't reach their ends.
Inputs may be any that keep to these rules, and one draw needn't show every extreme that they name: `labels`: among the rows of one device (aligned blocks of 128 rows) no label appears more than 8 times, and every such block has some label exactly 8 times.
All inputs are finite; a program needn't handle non-finite values.
Results may differ from the reference program's by a relative error of at most 0.0058.
Values may be sent and summed in bfloat16 or wider, within the bound.
No kernel may reach another device: no remote copies, remote signals or barrier semaphores. Data moves between devices by JAX's collectives and lax.ppermute only.
A program may use at most 320 MiB of HBM per device.

```python
import math
import jax
import jax.numpy as jnp
from jax import lax

D = 2048
FF = 4096
SPLIT = 2
NDOM = 22
TOK_DEV = 128
EXPERTS = 32
CAP = 8
TOKENS = 8192


def label_block(block_key):
    key_full, key_pick, key_order = jax.random.split(block_key, 3)
    total_slots = EXPERTS * CAP
    slot_ids = jnp.arange(total_slots, dtype=jnp.int32)
    slot_owner = slot_ids // CAP
    forced = jax.random.randint(key_full, (), 0, EXPERTS, dtype=jnp.int32)
    shuffled = jax.random.permutation(key_pick, slot_ids).astype(jnp.int32)
    priority = shuffled + jnp.where(slot_owner == forced, -total_slots, 0).astype(jnp.int32)
    picked = jnp.argsort(priority, stable=True)[:TOK_DEV].astype(jnp.int32)
    block_labels = picked // CAP
    order = jax.random.permutation(key_order, jnp.arange(TOK_DEV, dtype=jnp.int32))
    return block_labels[order].astype(jnp.int32)


def draw_labels(key, part):
    blocks = TOKENS // TOK_DEV
    block_keys = jax.random.split(jax.random.fold_in(key, 7), blocks)
    labels_all = jax.vmap(label_block)(block_keys)
    return labels_all.reshape(TOKENS, 1).astype(jnp.int32)


def touch_ends(values, own_key, low, top_value):
    index_at = [jax.random.randint(jax.random.fold_in(own_key, axis), (), 0, length) for axis, length in enumerate(values.shape)]
    main_axis = values.shape.index(max(values.shape))
    neighbour = index_at[:main_axis] + [(index_at[main_axis] + 1) % values.shape[main_axis]] + index_at[main_axis + 1:]
    return values.at[tuple(index_at)].set(low).at[tuple(neighbour)].set(top_value)


def block_levels(stream_key, extent, shards, smallest, top_value):
    level = 1.0
    for axis_at, blocks in shards:
        steps = jax.random.uniform(jax.random.fold_in(jax.random.fold_in(stream_key, 6), axis_at), (blocks,), jnp.float32, smallest / len(shards), top_value / len(shards))
        level = level * jnp.repeat(jnp.exp(steps), extent[axis_at] // blocks).reshape((-1,) + (1,) * (len(extent) - 1 - axis_at))
    return level


def centred(rng, shape, width, reach, cuts=(), kind=jnp.bfloat16):
    loudness = block_levels(rng, shape, cuts, -0.22, 0.18) if cuts else 1.0
    entries = jax.random.normal(rng, shape, jnp.float32) * width * loudness
    return jnp.minimum(jnp.maximum(entries, -reach), reach).astype(kind)


def setup_inputs(seed: int = 0) -> dict:
    arg_keys = jax.random.split(jax.random.key(seed), 9)
    return {
        "tokens": centred(arg_keys[0], (TOKENS, D), 1.0, 6.0, ((0, 64), (1, 4))),
        "labels": draw_labels(jax.random.fold_in(arg_keys[8], 71), 0),
        "domain_ids": touch_ends(jax.random.randint(arg_keys[2], (TOKENS,), 0, NDOM), jax.random.fold_in(arg_keys[2], 1), 0, NDOM - 1).astype(jnp.int32),
        "domain_weights": jnp.clip(jnp.exp(jax.random.uniform(arg_keys[3], (NDOM,), jnp.float32, math.log(0.02), math.log(0.5))), 0.02, 0.5),
        "cotangent": centred(arg_keys[4], (TOKENS, D), 1.0, 6.0, ((0, 64), (1, 4))),
        "gate_weight": centred(arg_keys[5], (EXPERTS * SPLIT, D, FF // SPLIT), D ** -0.5, 0.125, ((0, 64), (2, 4))),
        "up_weight": centred(arg_keys[6], (EXPERTS * SPLIT, D, FF // SPLIT), D ** -0.5, 0.125, ((0, 64), (2, 4))),
        "down_weight": centred(arg_keys[7], (EXPERTS * SPLIT, FF // SPLIT, D), FF ** -0.5, 0.09375, ((0, 64), (1, 4))),
    }


def silu_parts(gate_pre):
    squash = jax.nn.sigmoid(gate_pre)
    return squash, gate_pre * squash


def reference(tokens, labels, domain_ids, domain_weights, cotangent, gate_weight, up_weight, down_weight):
    lang_label = labels[:, 0]
    grad_rows = (domain_weights[domain_ids][:, None] * cotangent.astype(jnp.float32)).astype(jnp.bfloat16)
    blocks = TOKENS // TOK_DEV
    grouped = lang_label.reshape(blocks, TOK_DEV)
    positions = jnp.arange(TOK_DEV, dtype=jnp.int32)
    earlier = positions[None, :] < positions[:, None]
    same_label = grouped[:, :, None] == grouped[:, None, :]
    slot_pos = jnp.sum((same_label & earlier[None]).astype(jnp.int32), axis=2)
    position = (jnp.arange(blocks, dtype=jnp.int32)[:, None] * CAP + slot_pos).reshape(TOKENS).astype(jnp.int32)
    spill_row = blocks * CAP
    gate_all = gate_weight.reshape(EXPERTS, SPLIT, D, FF // SPLIT).transpose(0, 2, 1, 3).reshape(EXPERTS, D, FF)
    up_all = up_weight.reshape(EXPERTS, SPLIT, D, FF // SPLIT).transpose(0, 2, 1, 3).reshape(EXPERTS, D, FF)
    down_all = down_weight.reshape(EXPERTS, FF, D)

    def expert_step(running, pieces):
        out_sum, input_sum = running
        expert, w_gate, w_up, w_down = pieces
        chosen = lang_label == expert
        scatter_index = jnp.where(chosen, position, spill_row).astype(jnp.int32)
        routed = jnp.zeros((spill_row, D), jnp.bfloat16).at[scatter_index].set(tokens, mode="drop")
        routed_grad = jnp.zeros((spill_row, D), jnp.bfloat16).at[scatter_index].set(grad_rows, mode="drop")
        gate_pre = jnp.dot(routed, w_gate, preferred_element_type=jnp.float32)
        up_pre = jnp.dot(routed, w_up, preferred_element_type=jnp.float32)
        squash, activated = silu_parts(gate_pre)
        hidden = (activated * up_pre).astype(jnp.bfloat16)
        out_rows = jnp.dot(hidden, w_down, preferred_element_type=jnp.float32)
        grad_hidden = jnp.dot(routed_grad, w_down.T, preferred_element_type=jnp.float32)
        grad_gate_pre = (grad_hidden * up_pre * squash * (1.0 + gate_pre * (1.0 - squash))).astype(jnp.bfloat16)
        grad_up_pre = (grad_hidden * activated).astype(jnp.bfloat16)
        gate_part = jnp.dot(routed.T, grad_gate_pre, preferred_element_type=jnp.float32).astype(jnp.bfloat16)
        up_part = jnp.dot(routed.T, grad_up_pre, preferred_element_type=jnp.float32).astype(jnp.bfloat16)
        down_part = jnp.dot(hidden.T, routed_grad, preferred_element_type=jnp.float32).astype(jnp.bfloat16)
        input_rows = jnp.dot(grad_gate_pre, w_gate.T, preferred_element_type=jnp.float32) + jnp.dot(grad_up_pre, w_up.T, preferred_element_type=jnp.float32)
        zero_val = jnp.zeros((), jnp.float32)
        out_sum = out_sum + jnp.where(chosen[:, None], out_rows[position], zero_val)
        input_sum = input_sum + jnp.where(chosen[:, None], input_rows[position], zero_val)
        return (out_sum, input_sum), (gate_part, up_part, down_part)

    start = (jnp.zeros((TOKENS, D), jnp.float32), jnp.zeros((TOKENS, D), jnp.float32))
    xs_all = (jnp.arange(EXPERTS, dtype=jnp.int32), gate_all, up_all, down_all)
    (out_sum, input_sum), (gate_parts, up_parts, down_parts) = lax.scan(expert_step, start, xs_all)
    gate_grad = gate_parts.reshape(EXPERTS, D, SPLIT, FF // SPLIT).transpose(0, 2, 1, 3).reshape(EXPERTS * SPLIT, D, FF // SPLIT)
    up_grad = up_parts.reshape(EXPERTS, D, SPLIT, FF // SPLIT).transpose(0, 2, 1, 3).reshape(EXPERTS * SPLIT, D, FF // SPLIT)
    down_grad = down_parts.reshape(EXPERTS * SPLIT, FF // SPLIT, D)
    return (out_sum.astype(jnp.bfloat16), input_sum.astype(jnp.bfloat16), gate_grad, up_grad, down_grad)
```

```python
import jax
import jax.numpy as jnp
from jax import lax
from jax.sharding import PartitionSpec as P

SPLIT = 2


def partner(value, axis, stride):
    return lax.ppermute(value, axis, [(i, i ^ 1 << stride) for i in range(lax.axis_size(axis))])


def shifted(value, axis, step):
    size = lax.axis_size(axis)
    return lax.ppermute(value, axis, [(i, (i + step) % size) for i in range(size)])


def silu_parts(gate_pre):
    squash = jax.nn.sigmoid(gate_pre)
    return (squash, gate_pre * squash)


def body(
    tokens, labels, domain_ids, domain_weights, cotangent, gate_weight, up_weight, down_weight
):
    n_expert = lax.axis_size("expert")
    n_tensor = lax.axis_size("tensor")
    tok_rows = tokens.shape[0]
    feat_slice = tokens.shape[1]
    experts_all = n_expert // SPLIT
    capacity = SPLIT * tok_rows // experts_all
    half_cap = capacity // SPLIT
    t_idx = lax.axis_index("tensor")
    lang_label = labels[:, 0]
    dom_hot = (
        domain_ids[:, None] == jnp.arange(domain_weights.shape[0], dtype=jnp.int32)[None, :]
    ).astype(jnp.float32)
    tok_scale = jnp.sum(dom_hot * domain_weights[None, :], axis=1)
    grad_rows = (tok_scale[:, None] * cotangent.astype(jnp.float32)).astype(jnp.bfloat16)
    lab_hot = (lang_label[:, None] == jnp.arange(experts_all, dtype=jnp.int32)[None, :]).astype(
        jnp.float32
    )
    row_ids = jnp.arange(tok_rows, dtype=jnp.int32)
    earlier = (row_ids[None, :] < row_ids[:, None]).astype(jnp.float32)
    before = jnp.dot(earlier, lab_hot, precision=lax.Precision.HIGHEST)
    slot_pos = jnp.sum(before * lab_hot, axis=1).astype(jnp.int32)
    target_row = lang_label * capacity + slot_pos
    rows_out = n_expert * half_cap
    sources = jnp.stack((tokens, grad_rows))
    dispatch_map = (
        jnp.arange(rows_out, dtype=jnp.int32)[:, None] == target_row[None, :]
    ).astype(jnp.bfloat16)
    outbound = jnp.einsum(
        "rt,ktw->krw", dispatch_map, sources, preferred_element_type=jnp.float32
    ).astype(jnp.bfloat16)
    outbound = outbound.reshape(2, n_expert, half_cap, feat_slice)
    arrived = lax.all_to_all(outbound, "expert", split_axis=1, concat_axis=1, tiled=True)
    pieces = [arrived] + [shifted(arrived, "tensor", k) for k in range(1, n_tensor)]
    reversed_pieces = jnp.stack([pieces[(-m) % n_tensor] for m in range(n_tensor)])
    ordered = jnp.roll(reversed_pieces, t_idx, axis=0)
    own_rows = jnp.moveaxis(ordered, 0, 3).reshape(2, rows_out, n_tensor * feat_slice)
    other_rows = partner(own_rows, "expert", 0)
    routed_both = jnp.concatenate((own_rows, other_rows), axis=1)
    routed = routed_both[0]
    routed_grad = routed_both[1]
    w_gate = gate_weight[0]
    w_up = up_weight[0]
    w_down = down_weight[0]
    contract_rows = (((0,), (0,)), ((), ()))
    contract_cols = (((1,), (1,)), ((), ()))
    gate_pre = jnp.dot(routed, w_gate, preferred_element_type=jnp.float32)
    up_pre = jnp.dot(routed, w_up, preferred_element_type=jnp.float32)
    squash, activated = silu_parts(gate_pre)
    hidden = (activated * up_pre).astype(jnp.bfloat16)
    out_part = jnp.dot(hidden, w_down, preferred_element_type=jnp.float32)
    grad_hidden = lax.dot_general(
        routed_grad, w_down, contract_cols, preferred_element_type=jnp.float32
    )
    grad_gate_pre = (grad_hidden * up_pre * squash * (1.0 + gate_pre * (1.0 - squash))).astype(
        jnp.bfloat16
    )
    grad_up_pre = (grad_hidden * activated).astype(jnp.bfloat16)
    gate_grad = lax.dot_general(
        routed, grad_gate_pre, contract_rows, preferred_element_type=jnp.float32
    ).astype(jnp.bfloat16)[None]
    up_grad = lax.dot_general(
        routed, grad_up_pre, contract_rows, preferred_element_type=jnp.float32
    ).astype(jnp.bfloat16)[None]
    down_grad = lax.dot_general(
        hidden, routed_grad, contract_rows, preferred_element_type=jnp.float32
    ).astype(jnp.bfloat16)[None]
    input_part = lax.dot_general(
        grad_gate_pre, w_gate, contract_cols, preferred_element_type=jnp.float32
    ) + lax.dot_general(grad_up_pre, w_up, contract_cols, preferred_element_type=jnp.float32)
    partial_value = jnp.stack((out_part, input_part))
    core_sum = partial_value[:, :rows_out] + partner(partial_value[:, rows_out:], "expert", 0)
    chunks = core_sum.reshape(2, rows_out, n_tensor, feat_slice)
    acc = lax.dynamic_index_in_dim(chunks, t_idx, axis=2, keepdims=False)
    for k in range(1, n_tensor):
        sent = lax.dynamic_index_in_dim(chunks, (t_idx + k) % n_tensor, axis=2, keepdims=False)
        acc = acc + shifted(sent, "tensor", k)
    going_back = acc.astype(jnp.bfloat16).reshape(2, n_expert, half_cap, feat_slice)
    returned = lax.all_to_all(going_back, "expert", split_axis=1, concat_axis=1, tiled=True)
    flat_back = returned.reshape(2, rows_out, feat_slice)
    home_map = (
        jnp.arange(rows_out, dtype=jnp.int32)[:, None] == target_row[None, :]
    ).astype(jnp.bfloat16)
    gathered_home = jnp.einsum(
        "rt,krw->ktw", home_map, flat_back, preferred_element_type=jnp.float32
    ).astype(jnp.bfloat16)
    return (gathered_home[0], gathered_home[1], gate_grad, up_grad, down_grad)


def solution(mesh):
    return jax.shard_map(
        body,
        mesh=mesh,
        in_specs=(
            P("expert", "tensor"),
            P("expert", None),
            P("expert"),
            P(),
            P("expert", "tensor"),
            P("expert", None, "tensor"),
            P("expert", None, "tensor"),
            P("expert", "tensor", None),
        ),
        out_specs=(
            P("expert", "tensor"),
            P("expert", "tensor"),
            P("expert", None, "tensor"),
            P("expert", None, "tensor"),
            P("expert", "tensor", None),
        ),
        check_vma=False,
    )
```

```python
import jax
import jax.numpy as jnp
from jax import lax
from jax.sharding import PartitionSpec as P

SPLIT = 2


def partner(value, axis, stride):
    return lax.ppermute(value, axis, [(i, i ^ 1 << stride) for i in range(lax.axis_size(axis))])


def shifted(value, axis, step):
    size = lax.axis_size(axis)
    return lax.ppermute(value, axis, [(i, (i + step) % size) for i in range(size)])


def silu_parts(gate_pre):
    squash = jax.nn.sigmoid(gate_pre)
    return (squash, gate_pre * squash)


def body(
    tokens, labels, domain_ids, domain_weights, cotangent, gate_weight, up_weight, down_weight
):
    n_expert = lax.axis_size("expert")
    n_tensor = lax.axis_size("tensor")
    tok_rows = tokens.shape[0]
    feat_slice = tokens.shape[1]
    experts_all = n_expert // SPLIT
    capacity = SPLIT * tok_rows // experts_all
    half_cap = capacity // SPLIT
    t_idx = lax.axis_index("tensor")
    lang_label = labels[:, 0]
    dom_hot = (
        domain_ids[:, None] == jnp.arange(domain_weights.shape[0], dtype=jnp.int32)[None, :]
    ).astype(jnp.float32)
    tok_scale = jnp.sum(dom_hot * domain_weights[None, :], axis=1)
    grad_rows = (tok_scale[:, None] * cotangent.astype(jnp.float32)).astype(jnp.bfloat16)
    lab_hot = (lang_label[:, None] == jnp.arange(experts_all, dtype=jnp.int32)[None, :]).astype(
        jnp.float32
    )
    row_ids = jnp.arange(tok_rows, dtype=jnp.int32)
    earlier = (row_ids[None, :] < row_ids[:, None]).astype(jnp.float32)
    before = jnp.dot(earlier, lab_hot, precision=lax.Precision.HIGHEST)
    slot_pos = jnp.sum(before * lab_hot, axis=1).astype(jnp.int32)
    target_row = lang_label * capacity + slot_pos
    rows_out = n_expert * half_cap
    sources = jnp.stack((tokens, grad_rows))
    dispatch_map = (
        jnp.arange(rows_out, dtype=jnp.int32)[:, None] == target_row[None, :]
    ).astype(jnp.bfloat16)
    outbound = jnp.einsum(
        "rt,ktw->krw", dispatch_map, sources, preferred_element_type=jnp.float32
    ).astype(jnp.bfloat16)
    outbound = outbound.reshape(2, n_expert, half_cap, feat_slice)
    arrived = lax.all_to_all(outbound, "expert", split_axis=1, concat_axis=1, tiled=True)
    pieces = [arrived.reshape(2, rows_out, feat_slice)]
    pieces += [shifted(pieces[0], "tensor", k) for k in range(1, n_tensor)]
    blocks = [jnp.concatenate((p, partner(p, "expert", 0)), axis=1) for p in pieces]
    src_off = [((t_idx - k) % n_tensor) * feat_slice for k in range(n_tensor)]
    w_gate = gate_weight[0]
    w_up = up_weight[0]
    w_down = down_weight[0]
    contract_rows = (((0,), (0,)), ((), ()))
    contract_cols = (((1,), (1,)), ((), ()))

    def rows_of(w, off):
        return lax.dynamic_slice_in_dim(w, off, feat_slice, axis=0)

    def cols_of(w, off):
        return lax.dynamic_slice_in_dim(w, off, feat_slice, axis=1)

    def block_sum(terms):
        total = terms[0]
        for term in terms[1:]:
            total = total + term
        return total

    gate_pre = block_sum(
        [
            jnp.dot(b[0], rows_of(w_gate, o), preferred_element_type=jnp.float32)
            for b, o in zip(blocks, src_off)
        ]
    )
    up_pre = block_sum(
        [
            jnp.dot(b[0], rows_of(w_up, o), preferred_element_type=jnp.float32)
            for b, o in zip(blocks, src_off)
        ]
    )
    grad_hidden = block_sum(
        [
            lax.dot_general(
                b[1], cols_of(w_down, o), contract_cols, preferred_element_type=jnp.float32
            )
            for b, o in zip(blocks, src_off)
        ]
    )
    squash, activated = silu_parts(gate_pre)
    hidden = (activated * up_pre).astype(jnp.bfloat16)
    grad_gate_pre = (grad_hidden * up_pre * squash * (1.0 + gate_pre * (1.0 - squash))).astype(
        jnp.bfloat16
    )
    grad_up_pre = (grad_hidden * activated).astype(jnp.bfloat16)
    gate_grad = jnp.zeros(w_gate.shape, jnp.bfloat16)
    up_grad = jnp.zeros(w_up.shape, jnp.bfloat16)
    down_grad = jnp.zeros(w_down.shape, jnp.bfloat16)
    for b, o in zip(blocks, src_off):
        gate_piece = lax.dot_general(
            b[0], grad_gate_pre, contract_rows, preferred_element_type=jnp.float32
        ).astype(jnp.bfloat16)
        up_piece = lax.dot_general(
            b[0], grad_up_pre, contract_rows, preferred_element_type=jnp.float32
        ).astype(jnp.bfloat16)
        down_piece = lax.dot_general(
            hidden, b[1], contract_rows, preferred_element_type=jnp.float32
        ).astype(jnp.bfloat16)
        gate_grad = lax.dynamic_update_slice_in_dim(gate_grad, gate_piece, o, axis=0)
        up_grad = lax.dynamic_update_slice_in_dim(up_grad, up_piece, o, axis=0)
        down_grad = lax.dynamic_update_slice_in_dim(down_grad, down_piece, o, axis=1)
    gate_grad = gate_grad[None]
    up_grad = up_grad[None]
    down_grad = down_grad[None]
    acc = None
    for m in range(n_tensor):
        off = ((t_idx + m) % n_tensor) * feat_slice
        out_m = jnp.dot(hidden, cols_of(w_down, off), preferred_element_type=jnp.float32)
        in_m = lax.dot_general(
            grad_gate_pre, rows_of(w_gate, off), contract_cols, preferred_element_type=jnp.float32
        ) + lax.dot_general(
            grad_up_pre, rows_of(w_up, off), contract_cols, preferred_element_type=jnp.float32
        )
        part_m = jnp.stack((out_m, in_m))
        core_m = part_m[:, :rows_out] + partner(part_m[:, rows_out:], "expert", 0)
        if m == 0:
            acc = core_m
        else:
            acc = acc + shifted(core_m.astype(jnp.bfloat16), "tensor", m).astype(jnp.float32)
    going_back = acc.astype(jnp.bfloat16).reshape(2, n_expert, half_cap, feat_slice)
    returned = lax.all_to_all(going_back, "expert", split_axis=1, concat_axis=1, tiled=True)
    flat_back = returned.reshape(2, rows_out, feat_slice)
    home_map = (
        jnp.arange(rows_out, dtype=jnp.int32)[:, None] == target_row[None, :]
    ).astype(jnp.bfloat16)
    gathered_home = jnp.einsum(
        "rt,krw->ktw", home_map, flat_back, preferred_element_type=jnp.float32
    ).astype(jnp.bfloat16)
    return (gathered_home[0], gathered_home[1], gate_grad, up_grad, down_grad)


def solution(mesh):
    return jax.shard_map(
        body,
        mesh=mesh,
        in_specs=(
            P("expert", "tensor"),
            P("expert", None),
            P("expert"),
            P(),
            P("expert", "tensor"),
            P("expert", None, "tensor"),
            P("expert", None, "tensor"),
            P("expert", "tensor", None),
        ),
        out_specs=(
            P("expert", "tensor"),
            P("expert", "tensor"),
            P("expert", None, "tensor"),
            P("expert", None, "tensor"),
            P("expert", "tensor", None),
        ),
        check_vma=False,
    )
```

```python
import jax
import jax.numpy as jnp
from jax import lax
from jax.sharding import PartitionSpec as P

SPLIT = 2


def partner(value, axis, stride):
    return lax.ppermute(value, axis, [(i, i ^ 1 << stride) for i in range(lax.axis_size(axis))])


def shifted(value, axis, step):
    size = lax.axis_size(axis)
    return lax.ppermute(value, axis, [(i, (i + step) % size) for i in range(size)])


def silu_parts(gate_pre):
    squash = jax.nn.sigmoid(gate_pre)
    return (squash, gate_pre * squash)


def body(
    tokens, labels, domain_ids, domain_weights, cotangent, gate_weight, up_weight, down_weight
):
    n_expert = lax.axis_size("expert")
    n_tensor = lax.axis_size("tensor")
    tok_rows = tokens.shape[0]
    feat_slice = tokens.shape[1]
    experts_all = n_expert // SPLIT
    capacity = SPLIT * tok_rows // experts_all
    half_cap = capacity // SPLIT
    t_idx = lax.axis_index("tensor")
    lang_label = labels[:, 0]
    dom_hot = (
        domain_ids[:, None] == jnp.arange(domain_weights.shape[0], dtype=jnp.int32)[None, :]
    ).astype(jnp.float32)
    tok_scale = jnp.sum(dom_hot * domain_weights[None, :], axis=1)
    grad_rows = (tok_scale[:, None] * cotangent.astype(jnp.float32)).astype(jnp.bfloat16)
    lab_hot = (lang_label[:, None] == jnp.arange(experts_all, dtype=jnp.int32)[None, :]).astype(
        jnp.float32
    )
    row_ids = jnp.arange(tok_rows, dtype=jnp.int32)
    earlier = (row_ids[None, :] < row_ids[:, None]).astype(jnp.float32)
    before = jnp.dot(earlier, lab_hot, precision=lax.Precision.HIGHEST)
    slot_pos = jnp.sum(before * lab_hot, axis=1).astype(jnp.int32)
    target_row = lang_label * capacity + slot_pos
    rows_out = n_expert * half_cap
    sources = jnp.stack((tokens, grad_rows))
    dispatch_map = (
        jnp.arange(rows_out, dtype=jnp.int32)[:, None] == target_row[None, :]
    ).astype(jnp.bfloat16)
    outbound = jnp.einsum(
        "rt,ktw->krw", dispatch_map, sources, preferred_element_type=jnp.float32
    ).astype(jnp.bfloat16)
    outbound = outbound.reshape(2, n_expert, half_cap, feat_slice)
    arrived = lax.all_to_all(outbound, "expert", split_axis=1, concat_axis=1, tiled=True)
    pieces = [arrived.reshape(2, rows_out, feat_slice)]
    pieces += [shifted(pieces[0], "tensor", k) for k in range(1, n_tensor)]
    groups = [pieces, [partner(p, "expert", 0) for p in pieces]]
    src_off = [((t_idx - k) % n_tensor) * feat_slice for k in range(n_tensor)]
    w_gate = gate_weight[0]
    w_up = up_weight[0]
    w_down = down_weight[0]
    contract_rows = (((0,), (0,)), ((), ()))
    contract_cols = (((1,), (1,)), ((), ()))

    def rows_of(w, off):
        return lax.dynamic_slice_in_dim(w, off, feat_slice, axis=0)

    def cols_of(w, off):
        return lax.dynamic_slice_in_dim(w, off, feat_slice, axis=1)

    def block_sum(terms):
        total = terms[0]
        for term in terms[1:]:
            total = total + term
        return total

    acts = []
    for blocks in groups:
        gate_pre = block_sum(
            [
                jnp.dot(b[0], rows_of(w_gate, o), preferred_element_type=jnp.float32)
                for b, o in zip(blocks, src_off)
            ]
        )
        up_pre = block_sum(
            [
                jnp.dot(b[0], rows_of(w_up, o), preferred_element_type=jnp.float32)
                for b, o in zip(blocks, src_off)
            ]
        )
        grad_hidden = block_sum(
            [
                lax.dot_general(
                    b[1], cols_of(w_down, o), contract_cols, preferred_element_type=jnp.float32
                )
                for b, o in zip(blocks, src_off)
            ]
        )
        squash, activated = silu_parts(gate_pre)
        hidden = (activated * up_pre).astype(jnp.bfloat16)
        grad_gate_pre = (
            grad_hidden * up_pre * squash * (1.0 + gate_pre * (1.0 - squash))
        ).astype(jnp.bfloat16)
        grad_up_pre = (grad_hidden * activated).astype(jnp.bfloat16)
        acts.append((hidden, grad_gate_pre, grad_up_pre))

    def partials(act, off):
        hidden, grad_gate_pre, grad_up_pre = act
        out_m = jnp.dot(hidden, cols_of(w_down, off), preferred_element_type=jnp.float32)
        in_m = lax.dot_general(
            grad_gate_pre, rows_of(w_gate, off), contract_cols, preferred_element_type=jnp.float32
        ) + lax.dot_general(
            grad_up_pre, rows_of(w_up, off), contract_cols, preferred_element_type=jnp.float32
        )
        return jnp.stack((out_m, in_m))

    acc = None
    for m in range(n_tensor):
        off = ((t_idx + m) % n_tensor) * feat_slice
        core_m = partials(acts[0], off) + partner(partials(acts[1], off), "expert", 0)
        if m == 0:
            acc = core_m
        else:
            acc = acc + shifted(core_m.astype(jnp.bfloat16), "tensor", m).astype(jnp.float32)
    gate_grad = jnp.zeros(w_gate.shape, jnp.bfloat16)
    up_grad = jnp.zeros(w_up.shape, jnp.bfloat16)
    down_grad = jnp.zeros(w_down.shape, jnp.bfloat16)
    for k, o in enumerate(src_off):
        gate_piece = block_sum(
            [
                lax.dot_general(
                    g[k][0], a[1], contract_rows, preferred_element_type=jnp.float32
                )
                for g, a in zip(groups, acts)
            ]
        ).astype(jnp.bfloat16)
        up_piece = block_sum(
            [
                lax.dot_general(
                    g[k][0], a[2], contract_rows, preferred_element_type=jnp.float32
                )
                for g, a in zip(groups, acts)
            ]
        ).astype(jnp.bfloat16)
        down_piece = block_sum(
            [
                lax.dot_general(
                    a[0], g[k][1], contract_rows, preferred_element_type=jnp.float32
                )
                for g, a in zip(groups, acts)
            ]
        ).astype(jnp.bfloat16)
        gate_grad = lax.dynamic_update_slice_in_dim(gate_grad, gate_piece, o, axis=0)
        up_grad = lax.dynamic_update_slice_in_dim(up_grad, up_piece, o, axis=0)
        down_grad = lax.dynamic_update_slice_in_dim(down_grad, down_piece, o, axis=1)
    gate_grad = gate_grad[None]
    up_grad = up_grad[None]
    down_grad = down_grad[None]
    going_back = acc.astype(jnp.bfloat16).reshape(2, n_expert, half_cap, feat_slice)
    returned = lax.all_to_all(going_back, "expert", split_axis=1, concat_axis=1, tiled=True)
    flat_back = returned.reshape(2, rows_out, feat_slice)
    home_map = (
        jnp.arange(rows_out, dtype=jnp.int32)[:, None] == target_row[None, :]
    ).astype(jnp.bfloat16)
    gathered_home = jnp.einsum(
        "rt,krw->ktw", home_map, flat_back, preferred_element_type=jnp.float32
    ).astype(jnp.bfloat16)
    return (gathered_home[0], gathered_home[1], gate_grad, up_grad, down_grad)


def solution(mesh):
    return jax.shard_map(
        body,
        mesh=mesh,
        in_specs=(
            P("expert", "tensor"),
            P("expert", None),
            P("expert"),
            P(),
            P("expert", "tensor"),
            P("expert", None, "tensor"),
            P("expert", None, "tensor"),
            P("expert", "tensor", None),
        ),
        out_specs=(
            P("expert", "tensor"),
            P("expert", "tensor"),
            P("expert", None, "tensor"),
            P("expert", None, "tensor"),
            P("expert", "tensor", None),
        ),
        check_vma=False,
    )
```

```python
import jax
import jax.numpy as jnp
from jax import lax
from jax.sharding import PartitionSpec as P

SPLIT = 2


def partner(value, axis, stride):
    return lax.ppermute(value, axis, [(i, i ^ 1 << stride) for i in range(lax.axis_size(axis))])


def shifted(value, axis, step):
    size = lax.axis_size(axis)
    return lax.ppermute(value, axis, [(i, (i + step) % size) for i in range(size)])


def ring_send(value, step):
    size = lax.axis_size("tensor")
    if 2 * step != size:
        return shifted(value, "tensor", step)
    half = value.shape[1] // 2
    ahead = value[:, :half]
    behind = value[:, half:]
    for _ in range(step):
        ahead = shifted(ahead, "tensor", 1)
        behind = shifted(behind, "tensor", -1)
    return jnp.concatenate((ahead, behind), axis=1)


def silu_parts(gate_pre):
    squash = jax.nn.sigmoid(gate_pre)
    return (squash, gate_pre * squash)


def body(
    tokens, labels, domain_ids, domain_weights, cotangent, gate_weight, up_weight, down_weight
):
    n_expert = lax.axis_size("expert")
    n_tensor = lax.axis_size("tensor")
    tok_rows = tokens.shape[0]
    feat_slice = tokens.shape[1]
    experts_all = n_expert // SPLIT
    capacity = SPLIT * tok_rows // experts_all
    half_cap = capacity // SPLIT
    t_idx = lax.axis_index("tensor")
    lang_label = labels[:, 0]
    dom_hot = (
        domain_ids[:, None] == jnp.arange(domain_weights.shape[0], dtype=jnp.int32)[None, :]
    ).astype(jnp.float32)
    tok_scale = jnp.sum(dom_hot * domain_weights[None, :], axis=1)
    grad_rows = (tok_scale[:, None] * cotangent.astype(jnp.float32)).astype(jnp.bfloat16)
    lab_hot = (lang_label[:, None] == jnp.arange(experts_all, dtype=jnp.int32)[None, :]).astype(
        jnp.float32
    )
    row_ids = jnp.arange(tok_rows, dtype=jnp.int32)
    earlier = (row_ids[None, :] < row_ids[:, None]).astype(jnp.float32)
    before = jnp.dot(earlier, lab_hot, precision=lax.Precision.HIGHEST)
    slot_pos = jnp.sum(before * lab_hot, axis=1).astype(jnp.int32)
    target_row = lang_label * capacity + slot_pos
    rows_out = n_expert * half_cap
    sources = jnp.stack((tokens, grad_rows))
    dispatch_map = (
        jnp.arange(rows_out, dtype=jnp.int32)[:, None] == target_row[None, :]
    ).astype(jnp.bfloat16)
    outbound = jnp.einsum(
        "rt,ktw->krw", dispatch_map, sources, preferred_element_type=jnp.float32
    ).astype(jnp.bfloat16)
    outbound = outbound.reshape(2, n_expert, half_cap, feat_slice)
    arrived = lax.all_to_all(outbound, "expert", split_axis=1, concat_axis=1, tiled=True)
    pieces = [arrived.reshape(2, rows_out, feat_slice)]
    pieces += [ring_send(pieces[0], k) for k in range(1, n_tensor)]
    blocks = [jnp.concatenate((p, partner(p, "expert", 0)), axis=1) for p in pieces]
    src_off = [((t_idx - k) % n_tensor) * feat_slice for k in range(n_tensor)]
    w_gate = gate_weight[0]
    w_up = up_weight[0]
    w_down = down_weight[0]
    contract_rows = (((0,), (0,)), ((), ()))
    contract_cols = (((1,), (1,)), ((), ()))

    def rows_of(w, off):
        return lax.dynamic_slice_in_dim(w, off, feat_slice, axis=0)

    def cols_of(w, off):
        return lax.dynamic_slice_in_dim(w, off, feat_slice, axis=1)

    def block_sum(terms):
        total = terms[0]
        for term in terms[1:]:
            total = total + term
        return total

    gate_pre = block_sum(
        [
            jnp.dot(b[0], rows_of(w_gate, o), preferred_element_type=jnp.float32)
            for b, o in zip(blocks, src_off)
        ]
    )
    up_pre = block_sum(
        [
            jnp.dot(b[0], rows_of(w_up, o), preferred_element_type=jnp.float32)
            for b, o in zip(blocks, src_off)
        ]
    )
    grad_hidden = block_sum(
        [
            lax.dot_general(
                b[1], cols_of(w_down, o), contract_cols, preferred_element_type=jnp.float32
            )
            for b, o in zip(blocks, src_off)
        ]
    )
    squash, activated = silu_parts(gate_pre)
    hidden = (activated * up_pre).astype(jnp.bfloat16)
    grad_gate_pre = (grad_hidden * up_pre * squash * (1.0 + gate_pre * (1.0 - squash))).astype(
        jnp.bfloat16
    )
    grad_up_pre = (grad_hidden * activated).astype(jnp.bfloat16)
    gate_grad = jnp.zeros(w_gate.shape, jnp.bfloat16)
    up_grad = jnp.zeros(w_up.shape, jnp.bfloat16)
    down_grad = jnp.zeros(w_down.shape, jnp.bfloat16)
    for b, o in zip(blocks, src_off):
        gate_piece = lax.dot_general(
            b[0], grad_gate_pre, contract_rows, preferred_element_type=jnp.float32
        ).astype(jnp.bfloat16)
        up_piece = lax.dot_general(
            b[0], grad_up_pre, contract_rows, preferred_element_type=jnp.float32
        ).astype(jnp.bfloat16)
        down_piece = lax.dot_general(
            hidden, b[1], contract_rows, preferred_element_type=jnp.float32
        ).astype(jnp.bfloat16)
        gate_grad = lax.dynamic_update_slice_in_dim(gate_grad, gate_piece, o, axis=0)
        up_grad = lax.dynamic_update_slice_in_dim(up_grad, up_piece, o, axis=0)
        down_grad = lax.dynamic_update_slice_in_dim(down_grad, down_piece, o, axis=1)
    gate_grad = gate_grad[None]
    up_grad = up_grad[None]
    down_grad = down_grad[None]
    acc = None
    for m in range(n_tensor):
        off = ((t_idx + m) % n_tensor) * feat_slice
        out_m = jnp.dot(hidden, cols_of(w_down, off), preferred_element_type=jnp.float32)
        in_m = lax.dot_general(
            grad_gate_pre, rows_of(w_gate, off), contract_cols, preferred_element_type=jnp.float32
        ) + lax.dot_general(
            grad_up_pre, rows_of(w_up, off), contract_cols, preferred_element_type=jnp.float32
        )
        part_m = jnp.stack((out_m, in_m))
        core_m = part_m[:, :rows_out] + partner(part_m[:, rows_out:], "expert", 0)
        if m == 0:
            acc = core_m
        else:
            acc = acc + ring_send(core_m.astype(jnp.bfloat16), m).astype(jnp.float32)
    going_back = acc.astype(jnp.bfloat16).reshape(2, n_expert, half_cap, feat_slice)
    returned = lax.all_to_all(going_back, "expert", split_axis=1, concat_axis=1, tiled=True)
    flat_back = returned.reshape(2, rows_out, feat_slice)
    home_map = (
        jnp.arange(rows_out, dtype=jnp.int32)[:, None] == target_row[None, :]
    ).astype(jnp.bfloat16)
    gathered_home = jnp.einsum(
        "rt,krw->ktw", home_map, flat_back, preferred_element_type=jnp.float32
    ).astype(jnp.bfloat16)
    return (gathered_home[0], gathered_home[1], gate_grad, up_grad, down_grad)


def solution(mesh):
    return jax.shard_map(
        body,
        mesh=mesh,
        in_specs=(
            P("expert", "tensor"),
            P("expert", None),
            P("expert"),
            P(),
            P("expert", "tensor"),
            P("expert", None, "tensor"),
            P("expert", None, "tensor"),
            P("expert", "tensor", None),
        ),
        out_specs=(
            P("expert", "tensor"),
            P("expert", "tensor"),
            P("expert", None, "tensor"),
            P("expert", None, "tensor"),
            P("expert", "tensor", None),
        ),
        check_vma=False,
    )
```

```python
import jax
import jax.numpy as jnp
from jax import lax
from jax.sharding import PartitionSpec as P

SPLIT = 2


def partner(value, axis, stride):
    return lax.ppermute(value, axis, [(i, i ^ 1 << stride) for i in range(lax.axis_size(axis))])


def shifted(value, axis, step):
    size = lax.axis_size(axis)
    return lax.ppermute(value, axis, [(i, (i + step) % size) for i in range(size)])


def silu_parts(gate_pre):
    squash = jax.nn.sigmoid(gate_pre)
    return (squash, gate_pre * squash)


def body(
    tokens, labels, domain_ids, domain_weights, cotangent, gate_weight, up_weight, down_weight
):
    n_expert = lax.axis_size("expert")
    n_tensor = lax.axis_size("tensor")
    tok_rows = tokens.shape[0]
    feat_slice = tokens.shape[1]
    experts_all = n_expert // SPLIT
    capacity = SPLIT * tok_rows // experts_all
    half_cap = capacity // SPLIT
    t_idx = lax.axis_index("tensor")
    lang_label = labels[:, 0]
    dom_hot = (
        domain_ids[:, None] == jnp.arange(domain_weights.shape[0], dtype=jnp.int32)[None, :]
    ).astype(jnp.float32)
    tok_scale = jnp.sum(dom_hot * domain_weights[None, :], axis=1)
    grad_rows = (tok_scale[:, None] * cotangent.astype(jnp.float32)).astype(jnp.bfloat16)
    lab_hot = (lang_label[:, None] == jnp.arange(experts_all, dtype=jnp.int32)[None, :]).astype(
        jnp.float32
    )
    row_ids = jnp.arange(tok_rows, dtype=jnp.int32)
    earlier = (row_ids[None, :] < row_ids[:, None]).astype(jnp.float32)
    before = jnp.dot(earlier, lab_hot, precision=lax.Precision.HIGHEST)
    slot_pos = jnp.sum(before * lab_hot, axis=1).astype(jnp.int32)
    target_row = lang_label * capacity + slot_pos
    rows_out = n_expert * half_cap
    sources = jnp.stack((tokens, grad_rows))
    dispatch_map = (
        jnp.arange(rows_out, dtype=jnp.int32)[:, None] == target_row[None, :]
    ).astype(jnp.bfloat16)
    outbound = jnp.einsum(
        "rt,ktw->krw", dispatch_map, sources, preferred_element_type=jnp.float32
    ).astype(jnp.bfloat16)
    outbound = outbound.reshape(2, n_expert, half_cap, feat_slice)
    arrived = lax.all_to_all(outbound, "expert", split_axis=1, concat_axis=1, tiled=True)
    pieces = [arrived.reshape(2, rows_out, feat_slice)]
    pieces += [shifted(pieces[0], "tensor", k) for k in range(1, n_tensor)]
    blocks = []
    for p in pieces:
        q = partner(p, "expert", 0)
        blocks.append([jnp.concatenate((p[i], q[i]), axis=0) for i in range(2)])
    src_off = [((t_idx - k) % n_tensor) * feat_slice for k in range(n_tensor)]
    w_gate = gate_weight[0]
    w_up = up_weight[0]
    w_down = down_weight[0]
    contract_rows = (((0,), (0,)), ((), ()))
    contract_cols = (((1,), (1,)), ((), ()))

    def rows_of(w, off):
        return lax.dynamic_slice_in_dim(w, off, feat_slice, axis=0)

    def cols_of(w, off):
        return lax.dynamic_slice_in_dim(w, off, feat_slice, axis=1)

    def block_sum(terms):
        total = terms[0]
        for term in terms[1:]:
            total = total + term
        return total

    gate_pre = block_sum(
        [
            jnp.dot(b[0], rows_of(w_gate, o), preferred_element_type=jnp.float32)
            for b, o in zip(blocks, src_off)
        ]
    )
    up_pre = block_sum(
        [
            jnp.dot(b[0], rows_of(w_up, o), preferred_element_type=jnp.float32)
            for b, o in zip(blocks, src_off)
        ]
    )
    grad_hidden = block_sum(
        [
            lax.dot_general(
                b[1], cols_of(w_down, o), contract_cols, preferred_element_type=jnp.float32
            )
            for b, o in zip(blocks, src_off)
        ]
    )
    squash, activated = silu_parts(gate_pre)
    hidden = (activated * up_pre).astype(jnp.bfloat16)
    grad_gate_pre = (grad_hidden * up_pre * squash * (1.0 + gate_pre * (1.0 - squash))).astype(
        jnp.bfloat16
    )
    grad_up_pre = (grad_hidden * activated).astype(jnp.bfloat16)
    gate_grad = jnp.zeros(w_gate.shape, jnp.bfloat16)
    up_grad = jnp.zeros(w_up.shape, jnp.bfloat16)
    down_grad = jnp.zeros(w_down.shape, jnp.bfloat16)
    for b, o in zip(blocks, src_off):
        gate_piece = lax.dot_general(
            b[0], grad_gate_pre, contract_rows, preferred_element_type=jnp.float32
        ).astype(jnp.bfloat16)
        up_piece = lax.dot_general(
            b[0], grad_up_pre, contract_rows, preferred_element_type=jnp.float32
        ).astype(jnp.bfloat16)
        down_piece = lax.dot_general(
            hidden, b[1], contract_rows, preferred_element_type=jnp.float32
        ).astype(jnp.bfloat16)
        gate_grad = lax.dynamic_update_slice_in_dim(gate_grad, gate_piece, o, axis=0)
        up_grad = lax.dynamic_update_slice_in_dim(up_grad, up_piece, o, axis=0)
        down_grad = lax.dynamic_update_slice_in_dim(down_grad, down_piece, o, axis=1)
    gate_grad = gate_grad[None]
    up_grad = up_grad[None]
    down_grad = down_grad[None]
    acc = None
    for m in range(n_tensor):
        off = ((t_idx + m) % n_tensor) * feat_slice
        out_m = jnp.dot(hidden, cols_of(w_down, off), preferred_element_type=jnp.float32)
        in_m = lax.dot_general(
            grad_gate_pre, rows_of(w_gate, off), contract_cols, preferred_element_type=jnp.float32
        ) + lax.dot_general(
            grad_up_pre, rows_of(w_up, off), contract_cols, preferred_element_type=jnp.float32
        )
        part_m = jnp.stack((out_m, in_m))
        core_m = part_m[:, :rows_out] + partner(part_m[:, rows_out:], "expert", 0)
        if m == 0:
            acc = core_m
        else:
            acc = acc + shifted(core_m.astype(jnp.bfloat16), "tensor", m).astype(jnp.float32)
    going_back = acc.astype(jnp.bfloat16).reshape(2, n_expert, half_cap, feat_slice)
    returned = lax.all_to_all(going_back, "expert", split_axis=1, concat_axis=1, tiled=True)
    flat_back = returned.reshape(2, rows_out, feat_slice)
    home_map = (
        jnp.arange(rows_out, dtype=jnp.int32)[:, None] == target_row[None, :]
    ).astype(jnp.bfloat16)
    gathered_home = jnp.einsum(
        "rt,krw->ktw", home_map, flat_back, preferred_element_type=jnp.float32
    ).astype(jnp.bfloat16)
    return (gathered_home[0], gathered_home[1], gate_grad, up_grad, down_grad)


def solution(mesh):
    return jax.shard_map(
        body,
        mesh=mesh,
        in_specs=(
            P("expert", "tensor"),
            P("expert", None),
            P("expert"),
            P(),
            P("expert", "tensor"),
            P("expert", None, "tensor"),
            P("expert", None, "tensor"),
            P("expert", "tensor", None),
        ),
        out_specs=(
            P("expert", "tensor"),
            P("expert", "tensor"),
            P("expert", None, "tensor"),
            P("expert", None, "tensor"),
            P("expert", "tensor", None),
        ),
        check_vma=False,
    )
```

```python
import jax
import jax.numpy as jnp
from jax import lax
from jax.sharding import PartitionSpec as P

SPLIT = 2


def partner(value, axis, stride):
    return lax.ppermute(value, axis, [(i, i ^ 1 << stride) for i in range(lax.axis_size(axis))])


def shifted(value, axis, step):
    size = lax.axis_size(axis)
    return lax.ppermute(value, axis, [(i, (i + step) % size) for i in range(size)])


def ring_send(value, step):
    return shifted(value, "tensor", step)


def silu_parts(gate_pre):
    squash = jax.nn.sigmoid(gate_pre)
    return (squash, gate_pre * squash)


def body(
    tokens, labels, domain_ids, domain_weights, cotangent, gate_weight, up_weight, down_weight
):
    n_expert = lax.axis_size("expert")
    n_tensor = lax.axis_size("tensor")
    tok_rows = tokens.shape[0]
    feat_slice = tokens.shape[1]
    experts_all = n_expert // SPLIT
    capacity = SPLIT * tok_rows // experts_all
    half_cap = capacity // SPLIT
    t_idx = lax.axis_index("tensor")
    lang_label = labels[:, 0]
    dom_hot = (
        domain_ids[:, None] == jnp.arange(domain_weights.shape[0], dtype=jnp.int32)[None, :]
    ).astype(jnp.float32)
    tok_scale = jnp.sum(dom_hot * domain_weights[None, :], axis=1)
    grad_rows = (tok_scale[:, None] * cotangent.astype(jnp.float32)).astype(jnp.bfloat16)
    lab_hot = (lang_label[:, None] == jnp.arange(experts_all, dtype=jnp.int32)[None, :]).astype(
        jnp.float32
    )
    row_ids = jnp.arange(tok_rows, dtype=jnp.int32)
    earlier = (row_ids[None, :] < row_ids[:, None]).astype(jnp.float32)
    before = jnp.dot(earlier, lab_hot, precision=lax.Precision.HIGHEST)
    slot_pos = jnp.sum(before * lab_hot, axis=1).astype(jnp.int32)
    target_row = lang_label * capacity + slot_pos
    rows_out = n_expert * half_cap
    sources = jnp.stack((tokens, grad_rows))
    dispatch_map = (
        jnp.arange(rows_out, dtype=jnp.int32)[:, None] == target_row[None, :]
    ).astype(jnp.bfloat16)
    outbound = jnp.einsum(
        "rt,ktw->krw", dispatch_map, sources, preferred_element_type=jnp.float32
    ).astype(jnp.bfloat16)
    outbound = outbound.reshape(2, n_expert, half_cap, feat_slice)
    arrived = lax.all_to_all(outbound, "expert", split_axis=1, concat_axis=1, tiled=True)
    flat_in = arrived.reshape(2, rows_out, feat_slice)
    blocks = [[], []]
    for i in range(2):
        own = flat_in[i]
        for k in range(n_tensor):
            p = own if k == 0 else ring_send(own, k)
            blocks[i].append(jnp.concatenate((p, partner(p, "expert", 0)), axis=0))
    blocks = list(zip(blocks[0], blocks[1]))
    src_off = [((t_idx - k) % n_tensor) * feat_slice for k in range(n_tensor)]
    w_gate = gate_weight[0]
    w_up = up_weight[0]
    w_down = down_weight[0]
    contract_rows = (((0,), (0,)), ((), ()))
    contract_cols = (((1,), (1,)), ((), ()))

    def rows_of(w, off):
        return lax.dynamic_slice_in_dim(w, off, feat_slice, axis=0)

    def cols_of(w, off):
        return lax.dynamic_slice_in_dim(w, off, feat_slice, axis=1)

    def block_sum(terms):
        total = terms[0]
        for term in terms[1:]:
            total = total + term
        return total

    gate_pre = block_sum(
        [
            jnp.dot(b[0], rows_of(w_gate, o), preferred_element_type=jnp.float32)
            for b, o in zip(blocks, src_off)
        ]
    )
    up_pre = block_sum(
        [
            jnp.dot(b[0], rows_of(w_up, o), preferred_element_type=jnp.float32)
            for b, o in zip(blocks, src_off)
        ]
    )
    grad_hidden = block_sum(
        [
            lax.dot_general(
                b[1], cols_of(w_down, o), contract_cols, preferred_element_type=jnp.float32
            )
            for b, o in zip(blocks, src_off)
        ]
    )
    squash, activated = silu_parts(gate_pre)
    hidden = (activated * up_pre).astype(jnp.bfloat16)
    grad_gate_pre = (grad_hidden * up_pre * squash * (1.0 + gate_pre * (1.0 - squash))).astype(
        jnp.bfloat16
    )
    grad_up_pre = (grad_hidden * activated).astype(jnp.bfloat16)
    gate_grad = jnp.zeros(w_gate.shape, jnp.bfloat16)
    up_grad = jnp.zeros(w_up.shape, jnp.bfloat16)
    down_grad = jnp.zeros(w_down.shape, jnp.bfloat16)
    for b, o in zip(blocks, src_off):
        gate_piece = lax.dot_general(
            b[0], grad_gate_pre, contract_rows, preferred_element_type=jnp.float32
        ).astype(jnp.bfloat16)
        up_piece = lax.dot_general(
            b[0], grad_up_pre, contract_rows, preferred_element_type=jnp.float32
        ).astype(jnp.bfloat16)
        down_piece = lax.dot_general(
            hidden, b[1], contract_rows, preferred_element_type=jnp.float32
        ).astype(jnp.bfloat16)
        gate_grad = lax.dynamic_update_slice_in_dim(gate_grad, gate_piece, o, axis=0)
        up_grad = lax.dynamic_update_slice_in_dim(up_grad, up_piece, o, axis=0)
        down_grad = lax.dynamic_update_slice_in_dim(down_grad, down_piece, o, axis=1)
    gate_grad = gate_grad[None]
    up_grad = up_grad[None]
    down_grad = down_grad[None]
    def out_partial(off):
        return jnp.dot(hidden, cols_of(w_down, off), preferred_element_type=jnp.float32)

    def in_partial(off):
        return lax.dot_general(
            grad_gate_pre, rows_of(w_gate, off), contract_cols, preferred_element_type=jnp.float32
        ) + lax.dot_general(
            grad_up_pre, rows_of(w_up, off), contract_cols, preferred_element_type=jnp.float32
        )

    sums = []
    for partial_of in (out_partial, in_partial):
        acc = None
        for m in range(n_tensor):
            part_m = partial_of(((t_idx + m) % n_tensor) * feat_slice)
            core_m = part_m[:rows_out] + partner(part_m[rows_out:], "expert", 0)
            if m == 0:
                acc = core_m
            else:
                acc = acc + ring_send(core_m.astype(jnp.bfloat16), m).astype(jnp.float32)
        sums.append(acc)
    acc = jnp.stack(sums)
    going_back = acc.astype(jnp.bfloat16).reshape(2, n_expert, half_cap, feat_slice)
    returned = lax.all_to_all(going_back, "expert", split_axis=1, concat_axis=1, tiled=True)
    flat_back = returned.reshape(2, rows_out, feat_slice)
    home_map = (
        jnp.arange(rows_out, dtype=jnp.int32)[:, None] == target_row[None, :]
    ).astype(jnp.bfloat16)
    gathered_home = jnp.einsum(
        "rt,krw->ktw", home_map, flat_back, preferred_element_type=jnp.float32
    ).astype(jnp.bfloat16)
    return (gathered_home[0], gathered_home[1], gate_grad, up_grad, down_grad)


def solution(mesh):
    return jax.shard_map(
        body,
        mesh=mesh,
        in_specs=(
            P("expert", "tensor"),
            P("expert", None),
            P("expert"),
            P(),
            P("expert", "tensor"),
            P("expert", None, "tensor"),
            P("expert", None, "tensor"),
            P("expert", "tensor", None),
        ),
        out_specs=(
            P("expert", "tensor"),
            P("expert", "tensor"),
            P("expert", None, "tensor"),
            P("expert", None, "tensor"),
            P("expert", "tensor", None),
        ),
        check_vma=False,
    )
```

```python
import jax
import jax.numpy as jnp
from jax import lax
from jax.sharding import PartitionSpec as P

SPLIT = 2


def partner(value, axis, stride):
    return lax.ppermute(value, axis, [(i, i ^ 1 << stride) for i in range(lax.axis_size(axis))])


def shifted(value, axis, step):
    size = lax.axis_size(axis)
    return lax.ppermute(value, axis, [(i, (i + step) % size) for i in range(size)])


def silu_parts(gate_pre):
    squash = jax.nn.sigmoid(gate_pre)
    return (squash, gate_pre * squash)


def body(
    tokens, labels, domain_ids, domain_weights, cotangent, gate_weight, up_weight, down_weight
):
    n_expert = lax.axis_size("expert")
    n_tensor = lax.axis_size("tensor")
    tok_rows = tokens.shape[0]
    feat_slice = tokens.shape[1]
    experts_all = n_expert // SPLIT
    capacity = SPLIT * tok_rows // experts_all
    half_cap = capacity // SPLIT
    t_idx = lax.axis_index("tensor")
    lang_label = labels[:, 0]
    dom_hot = (
        domain_ids[:, None] == jnp.arange(domain_weights.shape[0], dtype=jnp.int32)[None, :]
    ).astype(jnp.float32)
    tok_scale = jnp.sum(dom_hot * domain_weights[None, :], axis=1)
    grad_rows = (tok_scale[:, None] * cotangent.astype(jnp.float32)).astype(jnp.bfloat16)
    lab_hot = (lang_label[:, None] == jnp.arange(experts_all, dtype=jnp.int32)[None, :]).astype(
        jnp.float32
    )
    row_ids = jnp.arange(tok_rows, dtype=jnp.int32)
    earlier = (row_ids[None, :] < row_ids[:, None]).astype(jnp.float32)
    before = jnp.dot(earlier, lab_hot, precision=lax.Precision.HIGHEST)
    slot_pos = jnp.sum(before * lab_hot, axis=1).astype(jnp.int32)
    target_row = lang_label * capacity + slot_pos
    rows_out = n_expert * half_cap
    sources = jnp.concatenate((tokens, grad_rows), axis=1)
    dispatch_map = (
        jnp.arange(rows_out, dtype=jnp.int32)[:, None] == target_row[None, :]
    ).astype(jnp.bfloat16)
    outbound = jnp.dot(dispatch_map, sources, preferred_element_type=jnp.float32).astype(
        jnp.bfloat16
    )
    outbound = outbound.reshape(n_expert, half_cap, 2 * feat_slice)
    arrived = lax.all_to_all(outbound, "expert", split_axis=0, concat_axis=0, tiled=True)
    pieces = [arrived.reshape(rows_out, 2 * feat_slice)]
    pieces += [shifted(pieces[0], "tensor", k) for k in range(1, n_tensor)]
    blocks = []
    for p in pieces:
        both = jnp.concatenate((p, partner(p, "expert", 0)), axis=0)
        blocks.append((both[:, :feat_slice], both[:, feat_slice:]))
    src_off = [((t_idx - k) % n_tensor) * feat_slice for k in range(n_tensor)]
    w_gate = gate_weight[0]
    w_up = up_weight[0]
    w_down = down_weight[0]
    contract_rows = (((0,), (0,)), ((), ()))
    contract_cols = (((1,), (1,)), ((), ()))

    def rows_of(w, off):
        return lax.dynamic_slice_in_dim(w, off, feat_slice, axis=0)

    def cols_of(w, off):
        return lax.dynamic_slice_in_dim(w, off, feat_slice, axis=1)

    def block_sum(terms):
        total = terms[0]
        for term in terms[1:]:
            total = total + term
        return total

    gate_pre = block_sum(
        [
            jnp.dot(b[0], rows_of(w_gate, o), preferred_element_type=jnp.float32)
            for b, o in zip(blocks, src_off)
        ]
    )
    up_pre = block_sum(
        [
            jnp.dot(b[0], rows_of(w_up, o), preferred_element_type=jnp.float32)
            for b, o in zip(blocks, src_off)
        ]
    )
    grad_hidden = block_sum(
        [
            lax.dot_general(
                b[1], cols_of(w_down, o), contract_cols, preferred_element_type=jnp.float32
            )
            for b, o in zip(blocks, src_off)
        ]
    )
    squash, activated = silu_parts(gate_pre)
    hidden = (activated * up_pre).astype(jnp.bfloat16)
    grad_gate_pre = (grad_hidden * up_pre * squash * (1.0 + gate_pre * (1.0 - squash))).astype(
        jnp.bfloat16
    )
    grad_up_pre = (grad_hidden * activated).astype(jnp.bfloat16)
    gate_grad = jnp.zeros(w_gate.shape, jnp.bfloat16)
    up_grad = jnp.zeros(w_up.shape, jnp.bfloat16)
    down_grad = jnp.zeros(w_down.shape, jnp.bfloat16)
    for b, o in zip(blocks, src_off):
        gate_piece = lax.dot_general(
            b[0], grad_gate_pre, contract_rows, preferred_element_type=jnp.float32
        ).astype(jnp.bfloat16)
        up_piece = lax.dot_general(
            b[0], grad_up_pre, contract_rows, preferred_element_type=jnp.float32
        ).astype(jnp.bfloat16)
        down_piece = lax.dot_general(
            hidden, b[1], contract_rows, preferred_element_type=jnp.float32
        ).astype(jnp.bfloat16)
        gate_grad = lax.dynamic_update_slice_in_dim(gate_grad, gate_piece, o, axis=0)
        up_grad = lax.dynamic_update_slice_in_dim(up_grad, up_piece, o, axis=0)
        down_grad = lax.dynamic_update_slice_in_dim(down_grad, down_piece, o, axis=1)
    gate_grad = gate_grad[None]
    up_grad = up_grad[None]
    down_grad = down_grad[None]
    acc = None
    for m in range(n_tensor):
        off = ((t_idx + m) % n_tensor) * feat_slice
        out_m = jnp.dot(hidden, cols_of(w_down, off), preferred_element_type=jnp.float32)
        in_m = lax.dot_general(
            grad_gate_pre, rows_of(w_gate, off), contract_cols, preferred_element_type=jnp.float32
        ) + lax.dot_general(
            grad_up_pre, rows_of(w_up, off), contract_cols, preferred_element_type=jnp.float32
        )
        part_m = jnp.concatenate((out_m, in_m), axis=1)
        core_m = part_m[:rows_out] + partner(part_m[rows_out:], "expert", 0)
        if m == 0:
            acc = core_m
        else:
            acc = acc + shifted(core_m.astype(jnp.bfloat16), "tensor", m).astype(jnp.float32)
    going_back = acc.astype(jnp.bfloat16).reshape(n_expert, half_cap, 2 * feat_slice)
    returned = lax.all_to_all(going_back, "expert", split_axis=0, concat_axis=0, tiled=True)
    flat_back = returned.reshape(rows_out, 2 * feat_slice)
    home_map = (
        jnp.arange(rows_out, dtype=jnp.int32)[:, None] == target_row[None, :]
    ).astype(jnp.bfloat16)
    home = [
        lax.dot_general(
            home_map, flat_back[:, i * feat_slice : (i + 1) * feat_slice], contract_rows,
            preferred_element_type=jnp.float32,
        ).astype(jnp.bfloat16)
        for i in range(2)
    ]
    return (home[0], home[1], gate_grad, up_grad, down_grad)


def solution(mesh):
    return jax.shard_map(
        body,
        mesh=mesh,
        in_specs=(
            P("expert", "tensor"),
            P("expert", None),
            P("expert"),
            P(),
            P("expert", "tensor"),
            P("expert", None, "tensor"),
            P("expert", None, "tensor"),
            P("expert", "tensor", None),
        ),
        out_specs=(
            P("expert", "tensor"),
            P("expert", "tensor"),
            P("expert", None, "tensor"),
            P("expert", None, "tensor"),
            P("expert", "tensor", None),
        ),
        check_vma=False,
    )
```

```python
import jax
import jax.numpy as jnp
from jax import lax
from jax.sharding import PartitionSpec as P

SPLIT = 2


def partner(value, axis, stride):
    return lax.ppermute(value, axis, [(i, i ^ 1 << stride) for i in range(lax.axis_size(axis))])


def shifted(value, axis, step):
    size = lax.axis_size(axis)
    return lax.ppermute(value, axis, [(i, (i + step) % size) for i in range(size)])


def silu_parts(gate_pre):
    squash = jax.nn.sigmoid(gate_pre)
    return (squash, gate_pre * squash)


def body(
    tokens, labels, domain_ids, domain_weights, cotangent, gate_weight, up_weight, down_weight
):
    n_expert = lax.axis_size("expert")
    n_tensor = lax.axis_size("tensor")
    tok_rows = tokens.shape[0]
    feat_slice = tokens.shape[1]
    experts_all = n_expert // SPLIT
    capacity = SPLIT * tok_rows // experts_all
    half_cap = capacity // SPLIT
    t_idx = lax.axis_index("tensor")
    lang_label = labels[:, 0]
    dom_hot = (
        domain_ids[:, None] == jnp.arange(domain_weights.shape[0], dtype=jnp.int32)[None, :]
    ).astype(jnp.float32)
    tok_scale = jnp.sum(dom_hot * domain_weights[None, :], axis=1)
    grad_rows = (tok_scale[:, None] * cotangent.astype(jnp.float32)).astype(jnp.bfloat16)
    lab_hot = (lang_label[:, None] == jnp.arange(experts_all, dtype=jnp.int32)[None, :]).astype(
        jnp.float32
    )
    row_ids = jnp.arange(tok_rows, dtype=jnp.int32)
    earlier = (row_ids[None, :] < row_ids[:, None]).astype(jnp.float32)
    before = jnp.dot(earlier, lab_hot, preferred_element_type=jnp.float32)
    slot_pos = jnp.sum(before * lab_hot, axis=1).astype(jnp.int32)
    target_row = lang_label * capacity + slot_pos
    rows_out = n_expert * half_cap
    sources = jnp.concatenate((tokens, grad_rows), axis=1)
    dispatch_map = (
        jnp.arange(rows_out, dtype=jnp.int32)[:, None] == target_row[None, :]
    ).astype(jnp.bfloat16)
    outbound = jnp.dot(dispatch_map, sources, preferred_element_type=jnp.float32).astype(
        jnp.bfloat16
    )
    outbound = outbound.reshape(n_expert, half_cap, 2 * feat_slice)
    arrived = lax.all_to_all(outbound, "expert", split_axis=0, concat_axis=0, tiled=True)
    own_piece = arrived.reshape(rows_out, 2 * feat_slice)
    order = sorted(range(n_tensor), key=lambda k: -min(k, n_tensor - k))
    received = {k: shifted(own_piece, "tensor", k) for k in order if k}
    order = [0] + [k for k in reversed(order) if k]
    pieces = [own_piece if k == 0 else received[k] for k in order]
    blocks = []
    for p in pieces:
        both = jnp.concatenate((p, partner(p, "expert", 0)), axis=0)
        blocks.append((both[:, :feat_slice], both[:, feat_slice:]))
    src_off = [((t_idx - k) % n_tensor) * feat_slice for k in order]
    w_gate = gate_weight[0]
    w_up = up_weight[0]
    w_down = down_weight[0]
    contract_rows = (((0,), (0,)), ((), ()))
    contract_cols = (((1,), (1,)), ((), ()))

    def rows_of(w, off):
        return lax.dynamic_slice_in_dim(w, off, feat_slice, axis=0)

    def cols_of(w, off):
        return lax.dynamic_slice_in_dim(w, off, feat_slice, axis=1)

    def block_sum(terms):
        total = terms[0]
        for term in terms[1:]:
            total = total + term
        return total

    gate_pre = block_sum(
        [
            jnp.dot(b[0], rows_of(w_gate, o), preferred_element_type=jnp.float32)
            for b, o in zip(blocks, src_off)
        ]
    )
    up_pre = block_sum(
        [
            jnp.dot(b[0], rows_of(w_up, o), preferred_element_type=jnp.float32)
            for b, o in zip(blocks, src_off)
        ]
    )
    grad_hidden = block_sum(
        [
            lax.dot_general(
                b[1], cols_of(w_down, o), contract_cols, preferred_element_type=jnp.float32
            )
            for b, o in zip(blocks, src_off)
        ]
    )
    squash, activated = silu_parts(gate_pre)
    hidden = (activated * up_pre).astype(jnp.bfloat16)
    grad_gate_pre = (grad_hidden * up_pre * squash * (1.0 + gate_pre * (1.0 - squash))).astype(
        jnp.bfloat16
    )
    grad_up_pre = (grad_hidden * activated).astype(jnp.bfloat16)
    gate_grad = jnp.zeros(w_gate.shape, jnp.bfloat16)
    up_grad = jnp.zeros(w_up.shape, jnp.bfloat16)
    down_grad = jnp.zeros(w_down.shape, jnp.bfloat16)
    for b, o in zip(blocks, src_off):
        gate_piece = lax.dot_general(
            b[0], grad_gate_pre, contract_rows, preferred_element_type=jnp.float32
        ).astype(jnp.bfloat16)
        up_piece = lax.dot_general(
            b[0], grad_up_pre, contract_rows, preferred_element_type=jnp.float32
        ).astype(jnp.bfloat16)
        down_piece = lax.dot_general(
            hidden, b[1], contract_rows, preferred_element_type=jnp.float32
        ).astype(jnp.bfloat16)
        gate_grad = lax.dynamic_update_slice_in_dim(gate_grad, gate_piece, o, axis=0)
        up_grad = lax.dynamic_update_slice_in_dim(up_grad, up_piece, o, axis=0)
        down_grad = lax.dynamic_update_slice_in_dim(down_grad, down_piece, o, axis=1)
    gate_grad = gate_grad[None]
    up_grad = up_grad[None]
    down_grad = down_grad[None]
    acc = None
    for m in sorted(range(n_tensor), key=lambda k: -min(k, n_tensor - k)):
        off = ((t_idx + m) % n_tensor) * feat_slice
        out_m = jnp.dot(hidden, cols_of(w_down, off), preferred_element_type=jnp.float32)
        in_m = lax.dot_general(
            grad_gate_pre, rows_of(w_gate, off), contract_cols, preferred_element_type=jnp.float32
        ) + lax.dot_general(
            grad_up_pre, rows_of(w_up, off), contract_cols, preferred_element_type=jnp.float32
        )
        part_m = jnp.concatenate((out_m, in_m), axis=1)
        core_m = part_m[:rows_out] + partner(part_m[rows_out:], "expert", 0)
        if m:
            core_m = shifted(core_m.astype(jnp.bfloat16), "tensor", m).astype(jnp.float32)
        acc = core_m if acc is None else acc + core_m
    going_back = acc.astype(jnp.bfloat16).reshape(n_expert, half_cap, 2 * feat_slice)
    returned = lax.all_to_all(going_back, "expert", split_axis=0, concat_axis=0, tiled=True)
    flat_back = returned.reshape(rows_out, 2 * feat_slice)
    home_map = (
        jnp.arange(rows_out, dtype=jnp.int32)[:, None] == target_row[None, :]
    ).astype(jnp.bfloat16)
    home = [
        lax.dot_general(
            home_map, flat_back[:, i * feat_slice : (i + 1) * feat_slice], contract_rows,
            preferred_element_type=jnp.float32,
        ).astype(jnp.bfloat16)
        for i in range(2)
    ]
    return (home[0], home[1], gate_grad, up_grad, down_grad)


def solution(mesh):
    return jax.shard_map(
        body,
        mesh=mesh,
        in_specs=(
            P("expert", "tensor"),
            P("expert", None),
            P("expert"),
            P(),
            P("expert", "tensor"),
            P("expert", None, "tensor"),
            P("expert", None, "tensor"),
            P("expert", "tensor", None),
        ),
        out_specs=(
            P("expert", "tensor"),
            P("expert", "tensor"),
            P("expert", None, "tensor"),
            P("expert", None, "tensor"),
            P("expert", "tensor", None),
        ),
        check_vma=False,
    )
```

```python
import jax
import jax.numpy as jnp
from jax import lax
from jax.sharding import PartitionSpec as P

SPLIT = 2


def partner(value, axis, stride):
    return lax.ppermute(value, axis, [(i, i ^ 1 << stride) for i in range(lax.axis_size(axis))])


def shifted(value, axis, step):
    size = lax.axis_size(axis)
    return lax.ppermute(value, axis, [(i, (i + step) % size) for i in range(size)])


def silu_parts(gate_pre):
    squash = jax.nn.sigmoid(gate_pre)
    return (squash, gate_pre * squash)


def body(
    tokens, labels, domain_ids, domain_weights, cotangent, gate_weight, up_weight, down_weight
):
    n_expert = lax.axis_size("expert")
    n_tensor = lax.axis_size("tensor")
    tok_rows = tokens.shape[0]
    feat_slice = tokens.shape[1]
    experts_all = n_expert // SPLIT
    capacity = SPLIT * tok_rows // experts_all
    half_cap = capacity // SPLIT
    t_idx = lax.axis_index("tensor")
    lang_label = labels[:, 0]
    dom_hot = (
        domain_ids[:, None] == jnp.arange(domain_weights.shape[0], dtype=jnp.int32)[None, :]
    ).astype(jnp.float32)
    tok_scale = jnp.sum(dom_hot * domain_weights[None, :], axis=1)
    grad_rows = (tok_scale[:, None] * cotangent.astype(jnp.float32)).astype(jnp.bfloat16)
    row_ids = jnp.arange(tok_rows, dtype=jnp.int32)
    same_before = (lang_label[None, :] == lang_label[:, None]) & (row_ids[None, :] < row_ids[:, None])
    slot_pos = jnp.sum(same_before.astype(jnp.int32), axis=1)
    target_row = lang_label * capacity + slot_pos
    rows_out = n_expert * half_cap
    sources = jnp.concatenate((tokens, grad_rows), axis=1)
    dispatch_map = (
        jnp.arange(rows_out, dtype=jnp.int32)[:, None] == target_row[None, :]
    ).astype(jnp.bfloat16)
    outbound = jnp.dot(dispatch_map, sources, preferred_element_type=jnp.float32).astype(
        jnp.bfloat16
    )
    outbound = outbound.reshape(n_expert, half_cap, 2 * feat_slice)
    arrived = lax.all_to_all(outbound, "expert", split_axis=0, concat_axis=0, tiled=True)
    own_piece = arrived.reshape(rows_out, 2 * feat_slice)
    order = sorted(range(n_tensor), key=lambda k: -min(k, n_tensor - k))
    received = {k: shifted(own_piece, "tensor", k) for k in order if k}
    order = [0] + [k for k in reversed(order) if k]
    pieces = [own_piece if k == 0 else received[k] for k in order]
    blocks = []
    for p in pieces:
        both = jnp.concatenate((p, partner(p, "expert", 0)), axis=0)
        blocks.append((both[:, :feat_slice], both[:, feat_slice:]))
    src_off = [((t_idx - k) % n_tensor) * feat_slice for k in order]
    w_gate = gate_weight[0]
    w_up = up_weight[0]
    w_down = down_weight[0]
    contract_rows = (((0,), (0,)), ((), ()))
    contract_cols = (((1,), (1,)), ((), ()))

    def rows_of(w, off):
        return lax.dynamic_slice_in_dim(w, off, feat_slice, axis=0)

    def cols_of(w, off):
        return lax.dynamic_slice_in_dim(w, off, feat_slice, axis=1)

    def block_sum(terms):
        total = terms[0]
        for term in terms[1:]:
            total = total + term
        return total

    gate_pre = block_sum(
        [
            jnp.dot(b[0], rows_of(w_gate, o), preferred_element_type=jnp.float32)
            for b, o in zip(blocks, src_off)
        ]
    )
    up_pre = block_sum(
        [
            jnp.dot(b[0], rows_of(w_up, o), preferred_element_type=jnp.float32)
            for b, o in zip(blocks, src_off)
        ]
    )
    grad_hidden = block_sum(
        [
            lax.dot_general(
                b[1], cols_of(w_down, o), contract_cols, preferred_element_type=jnp.float32
            )
            for b, o in zip(blocks, src_off)
        ]
    )
    squash, activated = silu_parts(gate_pre)
    hidden = (activated * up_pre).astype(jnp.bfloat16)
    grad_gate_pre = (grad_hidden * up_pre * squash * (1.0 + gate_pre * (1.0 - squash))).astype(
        jnp.bfloat16
    )
    grad_up_pre = (grad_hidden * activated).astype(jnp.bfloat16)
    gate_grad = jnp.zeros(w_gate.shape, jnp.bfloat16)
    up_grad = jnp.zeros(w_up.shape, jnp.bfloat16)
    down_grad = jnp.zeros(w_down.shape, jnp.bfloat16)
    for b, o in zip(blocks, src_off):
        gate_piece = lax.dot_general(
            b[0], grad_gate_pre, contract_rows, preferred_element_type=jnp.float32
        ).astype(jnp.bfloat16)
        up_piece = lax.dot_general(
            b[0], grad_up_pre, contract_rows, preferred_element_type=jnp.float32
        ).astype(jnp.bfloat16)
        down_piece = lax.dot_general(
            hidden, b[1], contract_rows, preferred_element_type=jnp.float32
        ).astype(jnp.bfloat16)
        gate_grad = lax.dynamic_update_slice_in_dim(gate_grad, gate_piece, o, axis=0)
        up_grad = lax.dynamic_update_slice_in_dim(up_grad, up_piece, o, axis=0)
        down_grad = lax.dynamic_update_slice_in_dim(down_grad, down_piece, o, axis=1)
    gate_grad = gate_grad[None]
    up_grad = up_grad[None]
    down_grad = down_grad[None]
    acc = None
    for m in sorted(range(n_tensor), key=lambda k: -min(k, n_tensor - k)):
        off = ((t_idx + m) % n_tensor) * feat_slice
        out_m = jnp.dot(hidden, cols_of(w_down, off), preferred_element_type=jnp.float32)
        in_m = lax.dot_general(
            grad_gate_pre, rows_of(w_gate, off), contract_cols, preferred_element_type=jnp.float32
        ) + lax.dot_general(
            grad_up_pre, rows_of(w_up, off), contract_cols, preferred_element_type=jnp.float32
        )
        part_m = jnp.concatenate((out_m, in_m), axis=1)
        handed = partner(part_m[rows_out:].astype(jnp.bfloat16), "expert", 0)
        core_m = part_m[:rows_out] + handed.astype(jnp.float32)
        if m:
            core_m = shifted(core_m.astype(jnp.bfloat16), "tensor", m).astype(jnp.float32)
        acc = core_m if acc is None else acc + core_m
    going_back = acc.astype(jnp.bfloat16).reshape(n_expert, half_cap, 2 * feat_slice)
    returned = lax.all_to_all(going_back, "expert", split_axis=0, concat_axis=0, tiled=True)
    flat_back = returned.reshape(rows_out, 2 * feat_slice)
    home_map = (
        jnp.arange(rows_out, dtype=jnp.int32)[:, None] == target_row[None, :]
    ).astype(jnp.bfloat16)
    home = [
        lax.dot_general(
            home_map, flat_back[:, i * feat_slice : (i + 1) * feat_slice], contract_rows,
            preferred_element_type=jnp.float32,
        ).astype(jnp.bfloat16)
        for i in range(2)
    ]
    return (home[0], home[1], gate_grad, up_grad, down_grad)


def solution(mesh):
    return jax.shard_map(
        body,
        mesh=mesh,
        in_specs=(
            P("expert", "tensor"),
            P("expert", None),
            P("expert"),
            P(),
            P("expert", "tensor"),
            P("expert", None, "tensor"),
            P("expert", None, "tensor"),
            P("expert", "tensor", None),
        ),
        out_specs=(
            P("expert", "tensor"),
            P("expert", "tensor"),
            P("expert", None, "tensor"),
            P("expert", None, "tensor"),
            P("expert", "tensor", None),
        ),
        check_vma=False,
    )
```

```python
import jax
import jax.numpy as jnp
from jax import lax
from jax.sharding import PartitionSpec as P

SPLIT = 2


def partner(value, axis, stride):
    return lax.ppermute(value, axis, [(i, i ^ 1 << stride) for i in range(lax.axis_size(axis))])


def shifted(value, axis, step):
    size = lax.axis_size(axis)
    return lax.ppermute(value, axis, [(i, (i + step) % size) for i in range(size)])


def silu_parts(gate_pre):
    squash = jax.nn.sigmoid(gate_pre)
    return (squash, gate_pre * squash)


def body(
    tokens, labels, domain_ids, domain_weights, cotangent, gate_weight, up_weight, down_weight
):
    n_expert = lax.axis_size("expert")
    n_tensor = lax.axis_size("tensor")
    tok_rows = tokens.shape[0]
    feat_slice = tokens.shape[1]
    experts_all = n_expert // SPLIT
    capacity = SPLIT * tok_rows // experts_all
    half_cap = capacity // SPLIT
    t_idx = lax.axis_index("tensor")
    lang_label = labels[:, 0]
    dom_hot = (
        domain_ids[:, None] == jnp.arange(domain_weights.shape[0], dtype=jnp.int32)[None, :]
    ).astype(jnp.float32)
    tok_scale = jnp.sum(dom_hot * domain_weights[None, :], axis=1)
    grad_rows = (tok_scale[:, None] * cotangent.astype(jnp.float32)).astype(jnp.bfloat16)
    lab_hot = (lang_label[:, None] == jnp.arange(experts_all, dtype=jnp.int32)[None, :]).astype(
        jnp.float32
    )
    row_ids = jnp.arange(tok_rows, dtype=jnp.int32)
    earlier = (row_ids[None, :] < row_ids[:, None]).astype(jnp.float32)
    before = jnp.dot(earlier, lab_hot, preferred_element_type=jnp.float32)
    slot_pos = jnp.sum(before * lab_hot, axis=1).astype(jnp.int32)
    target_row = lang_label * capacity + slot_pos
    rows_out = n_expert * half_cap
    w_gate = jnp.concatenate((gate_weight[0], partner(gate_weight[0], "expert", 0)), axis=1)
    w_up = jnp.concatenate((up_weight[0], partner(up_weight[0], "expert", 0)), axis=1)
    w_down = jnp.concatenate((down_weight[0], partner(down_weight[0], "expert", 0)), axis=0)
    hid_own = gate_weight.shape[2]
    sources = jnp.concatenate((tokens, grad_rows), axis=1)
    dispatch_map = (
        jnp.arange(rows_out, dtype=jnp.int32)[:, None] == target_row[None, :]
    ).astype(jnp.bfloat16)
    outbound = jnp.dot(dispatch_map, sources, preferred_element_type=jnp.float32).astype(
        jnp.bfloat16
    )
    outbound = outbound.reshape(n_expert, half_cap, 2 * feat_slice)
    arrived = lax.all_to_all(outbound, "expert", split_axis=0, concat_axis=0, tiled=True)
    own_piece = arrived.reshape(rows_out, 2 * feat_slice)
    order = sorted(range(n_tensor), key=lambda k: -min(k, n_tensor - k))
    received = {k: shifted(own_piece, "tensor", k) for k in order if k}
    order = [0] + [k for k in reversed(order) if k]
    pieces = [own_piece if k == 0 else received[k] for k in order]
    blocks = [(p[:, :feat_slice], p[:, feat_slice:]) for p in pieces]
    src_off = [((t_idx - k) % n_tensor) * feat_slice for k in order]
    contract_rows = (((0,), (0,)), ((), ()))
    contract_cols = (((1,), (1,)), ((), ()))

    def rows_of(w, off):
        return lax.dynamic_slice_in_dim(w, off, feat_slice, axis=0)

    def cols_of(w, off):
        return lax.dynamic_slice_in_dim(w, off, feat_slice, axis=1)

    def block_sum(terms):
        total = terms[0]
        for term in terms[1:]:
            total = total + term
        return total

    gate_pre = block_sum(
        [
            jnp.dot(b[0], rows_of(w_gate, o), preferred_element_type=jnp.float32)
            for b, o in zip(blocks, src_off)
        ]
    )
    up_pre = block_sum(
        [
            jnp.dot(b[0], rows_of(w_up, o), preferred_element_type=jnp.float32)
            for b, o in zip(blocks, src_off)
        ]
    )
    grad_hidden = block_sum(
        [
            lax.dot_general(
                b[1], cols_of(w_down, o), contract_cols, preferred_element_type=jnp.float32
            )
            for b, o in zip(blocks, src_off)
        ]
    )
    squash, activated = silu_parts(gate_pre)
    hidden = (activated * up_pre).astype(jnp.bfloat16)
    grad_gate_pre = (grad_hidden * up_pre * squash * (1.0 + gate_pre * (1.0 - squash))).astype(
        jnp.bfloat16
    )
    grad_up_pre = (grad_hidden * activated).astype(jnp.bfloat16)
    acc = None
    for m in sorted(range(n_tensor), key=lambda k: -min(k, n_tensor - k)):
        off = ((t_idx + m) % n_tensor) * feat_slice
        out_m = jnp.dot(hidden, cols_of(w_down, off), preferred_element_type=jnp.float32)
        in_m = lax.dot_general(
            grad_gate_pre, rows_of(w_gate, off), contract_cols, preferred_element_type=jnp.float32
        ) + lax.dot_general(
            grad_up_pre, rows_of(w_up, off), contract_cols, preferred_element_type=jnp.float32
        )
        core_m = jnp.concatenate((out_m, in_m), axis=1)
        if m:
            core_m = shifted(core_m.astype(jnp.bfloat16), "tensor", m).astype(jnp.float32)
        acc = core_m if acc is None else acc + core_m
    gate_both = jnp.zeros(w_gate.shape, jnp.float32)
    up_both = jnp.zeros(w_up.shape, jnp.float32)
    down_both = jnp.zeros(w_down.shape, jnp.float32)
    for b, o in zip(blocks, src_off):
        gate_piece = lax.dot_general(
            b[0], grad_gate_pre, contract_rows, preferred_element_type=jnp.float32
        )
        up_piece = lax.dot_general(
            b[0], grad_up_pre, contract_rows, preferred_element_type=jnp.float32
        )
        down_piece = lax.dot_general(
            hidden, b[1], contract_rows, preferred_element_type=jnp.float32
        )
        gate_both = lax.dynamic_update_slice_in_dim(gate_both, gate_piece, o, axis=0)
        up_both = lax.dynamic_update_slice_in_dim(up_both, up_piece, o, axis=0)
        down_both = lax.dynamic_update_slice_in_dim(down_both, down_piece, o, axis=1)
    gate_grad = (
        gate_both[:, :hid_own] + partner(gate_both[:, hid_own:], "expert", 0)
    ).astype(jnp.bfloat16)[None]
    up_grad = (up_both[:, :hid_own] + partner(up_both[:, hid_own:], "expert", 0)).astype(
        jnp.bfloat16
    )[None]
    down_grad = (
        down_both[:hid_own] + partner(down_both[hid_own:], "expert", 0)
    ).astype(jnp.bfloat16)[None]
    going_back = acc.astype(jnp.bfloat16).reshape(n_expert, half_cap, 2 * feat_slice)
    returned = lax.all_to_all(going_back, "expert", split_axis=0, concat_axis=0, tiled=True)
    flat_back = returned.reshape(rows_out, 2 * feat_slice)
    home_map = (
        jnp.arange(rows_out, dtype=jnp.int32)[:, None] == target_row[None, :]
    ).astype(jnp.bfloat16)
    home = [
        lax.dot_general(
            home_map, flat_back[:, i * feat_slice : (i + 1) * feat_slice], contract_rows,
            preferred_element_type=jnp.float32,
        ).astype(jnp.bfloat16)
        for i in range(2)
    ]
    return (home[0], home[1], gate_grad, up_grad, down_grad)


def solution(mesh):
    return jax.shard_map(
        body,
        mesh=mesh,
        in_specs=(
            P("expert", "tensor"),
            P("expert", None),
            P("expert"),
            P(),
            P("expert", "tensor"),
            P("expert", None, "tensor"),
            P("expert", None, "tensor"),
            P("expert", "tensor", None),
        ),
        out_specs=(
            P("expert", "tensor"),
            P("expert", "tensor"),
            P("expert", None, "tensor"),
            P("expert", None, "tensor"),
            P("expert", "tensor", None),
        ),
        check_vma=False,
    )
```

```python
import jax
import jax.numpy as jnp
from jax import lax
from jax.sharding import PartitionSpec as P

SPLIT = 2


def partner(value, axis, stride):
    return lax.ppermute(value, axis, [(i, i ^ 1 << stride) for i in range(lax.axis_size(axis))])


def shifted(value, axis, step):
    size = lax.axis_size(axis)
    return lax.ppermute(value, axis, [(i, (i + step) % size) for i in range(size)])


def silu_parts(gate_pre):
    squash = jax.nn.sigmoid(gate_pre)
    return (squash, gate_pre * squash)


def body(
    tokens, labels, domain_ids, domain_weights, cotangent, gate_weight, up_weight, down_weight
):
    n_expert = lax.axis_size("expert")
    n_tensor = lax.axis_size("tensor")
    tok_rows = tokens.shape[0]
    feat_slice = tokens.shape[1]
    experts_all = n_expert // SPLIT
    capacity = SPLIT * tok_rows // experts_all
    half_cap = capacity // SPLIT
    t_idx = lax.axis_index("tensor")
    lang_label = labels[:, 0]
    dom_hot = (
        domain_ids[:, None] == jnp.arange(domain_weights.shape[0], dtype=jnp.int32)[None, :]
    ).astype(jnp.float32)
    tok_scale = jnp.sum(dom_hot * domain_weights[None, :], axis=1)
    grad_rows = (tok_scale[:, None] * cotangent.astype(jnp.float32)).astype(jnp.bfloat16)
    lab_hot = (lang_label[:, None] == jnp.arange(experts_all, dtype=jnp.int32)[None, :]).astype(
        jnp.float32
    )
    row_ids = jnp.arange(tok_rows, dtype=jnp.int32)
    earlier = (row_ids[None, :] < row_ids[:, None]).astype(jnp.float32)
    before = jnp.dot(earlier, lab_hot, preferred_element_type=jnp.float32)
    slot_pos = jnp.sum(before * lab_hot, axis=1).astype(jnp.int32)
    target_row = lang_label * capacity + slot_pos
    rows_out = n_expert * half_cap
    sources = jnp.concatenate((tokens, grad_rows), axis=1)
    dispatch_map = (
        jnp.arange(rows_out, dtype=jnp.int32)[:, None] == target_row[None, :]
    ).astype(jnp.bfloat16)
    outbound = jnp.dot(dispatch_map, sources, preferred_element_type=jnp.float32).astype(
        jnp.bfloat16
    )
    outbound = outbound.reshape(n_expert, half_cap, 2 * feat_slice)
    arrived = lax.all_to_all(outbound, "expert", split_axis=0, concat_axis=0, tiled=True)
    own_piece = arrived.reshape(rows_out, 2 * feat_slice)
    order = sorted(range(n_tensor), key=lambda k: -min(k, n_tensor - k))
    received = {k: shifted(own_piece, "tensor", k) for k in order if k}
    order = [0] + [k for k in reversed(order) if k]
    pieces = [own_piece if k == 0 else received[k] for k in order]
    late = partner(jnp.stack(pieces[1:]), "expert", 0)
    swapped = [partner(pieces[0], "expert", 0)] + [late[i] for i in range(n_tensor - 1)]
    blocks = []
    for p, q in zip(pieces, swapped):
        both = jnp.concatenate((p, q), axis=0)
        blocks.append((both[:, :feat_slice], both[:, feat_slice:]))
    src_off = [((t_idx - k) % n_tensor) * feat_slice for k in order]
    w_gate = gate_weight[0]
    w_up = up_weight[0]
    w_down = down_weight[0]
    contract_rows = (((0,), (0,)), ((), ()))
    contract_cols = (((1,), (1,)), ((), ()))

    def rows_of(w, off):
        return lax.dynamic_slice_in_dim(w, off, feat_slice, axis=0)

    def cols_of(w, off):
        return lax.dynamic_slice_in_dim(w, off, feat_slice, axis=1)

    def block_sum(terms):
        total = terms[0]
        for term in terms[1:]:
            total = total + term
        return total

    gate_pre = block_sum(
        [
            jnp.dot(b[0], rows_of(w_gate, o), preferred_element_type=jnp.float32)
            for b, o in zip(blocks, src_off)
        ]
    )
    up_pre = block_sum(
        [
            jnp.dot(b[0], rows_of(w_up, o), preferred_element_type=jnp.float32)
            for b, o in zip(blocks, src_off)
        ]
    )
    grad_hidden = block_sum(
        [
            lax.dot_general(
                b[1], cols_of(w_down, o), contract_cols, preferred_element_type=jnp.float32
            )
            for b, o in zip(blocks, src_off)
        ]
    )
    squash, activated = silu_parts(gate_pre)
    hidden = (activated * up_pre).astype(jnp.bfloat16)
    grad_gate_pre = (grad_hidden * up_pre * squash * (1.0 + gate_pre * (1.0 - squash))).astype(
        jnp.bfloat16
    )
    grad_up_pre = (grad_hidden * activated).astype(jnp.bfloat16)
    gate_grad = jnp.zeros(w_gate.shape, jnp.bfloat16)
    up_grad = jnp.zeros(w_up.shape, jnp.bfloat16)
    down_grad = jnp.zeros(w_down.shape, jnp.bfloat16)
    for b, o in zip(blocks, src_off):
        gate_piece = lax.dot_general(
            b[0], grad_gate_pre, contract_rows, preferred_element_type=jnp.float32
        ).astype(jnp.bfloat16)
        up_piece = lax.dot_general(
            b[0], grad_up_pre, contract_rows, preferred_element_type=jnp.float32
        ).astype(jnp.bfloat16)
        down_piece = lax.dot_general(
            hidden, b[1], contract_rows, preferred_element_type=jnp.float32
        ).astype(jnp.bfloat16)
        gate_grad = lax.dynamic_update_slice_in_dim(gate_grad, gate_piece, o, axis=0)
        up_grad = lax.dynamic_update_slice_in_dim(up_grad, up_piece, o, axis=0)
        down_grad = lax.dynamic_update_slice_in_dim(down_grad, down_piece, o, axis=1)
    gate_grad = gate_grad[None]
    up_grad = up_grad[None]
    down_grad = down_grad[None]
    acc = None
    for m in sorted(range(n_tensor), key=lambda k: -min(k, n_tensor - k)):
        off = ((t_idx + m) % n_tensor) * feat_slice
        out_m = jnp.dot(hidden, cols_of(w_down, off), preferred_element_type=jnp.float32)
        in_m = lax.dot_general(
            grad_gate_pre, rows_of(w_gate, off), contract_cols, preferred_element_type=jnp.float32
        ) + lax.dot_general(
            grad_up_pre, rows_of(w_up, off), contract_cols, preferred_element_type=jnp.float32
        )
        part_m = jnp.concatenate((out_m, in_m), axis=1)
        core_m = part_m[:rows_out] + partner(part_m[rows_out:], "expert", 0)
        if m:
            core_m = shifted(core_m.astype(jnp.bfloat16), "tensor", m).astype(jnp.float32)
        acc = core_m if acc is None else acc + core_m
    going_back = acc.astype(jnp.bfloat16).reshape(n_expert, half_cap, 2 * feat_slice)
    returned = lax.all_to_all(going_back, "expert", split_axis=0, concat_axis=0, tiled=True)
    flat_back = returned.reshape(rows_out, 2 * feat_slice)
    home_map = (
        jnp.arange(rows_out, dtype=jnp.int32)[:, None] == target_row[None, :]
    ).astype(jnp.bfloat16)
    home = [
        lax.dot_general(
            home_map, flat_back[:, i * feat_slice : (i + 1) * feat_slice], contract_rows,
            preferred_element_type=jnp.float32,
        ).astype(jnp.bfloat16)
        for i in range(2)
    ]
    return (home[0], home[1], gate_grad, up_grad, down_grad)


def solution(mesh):
    return jax.shard_map(
        body,
        mesh=mesh,
        in_specs=(
            P("expert", "tensor"),
            P("expert", None),
            P("expert"),
            P(),
            P("expert", "tensor"),
            P("expert", None, "tensor"),
            P("expert", None, "tensor"),
            P("expert", "tensor", None),
        ),
        out_specs=(
            P("expert", "tensor"),
            P("expert", "tensor"),
            P("expert", None, "tensor"),
            P("expert", None, "tensor"),
            P("expert", "tensor", None),
        ),
        check_vma=False,
    )
```

```python
import jax
import jax.numpy as jnp
from jax import lax
from jax.sharding import PartitionSpec as P

SPLIT = 2


def partner(value, axis, stride):
    return lax.ppermute(value, axis, [(i, i ^ 1 << stride) for i in range(lax.axis_size(axis))])


def shifted(value, axis, step):
    size = lax.axis_size(axis)
    return lax.ppermute(value, axis, [(i, (i + step) % size) for i in range(size)])


def silu_parts(gate_pre):
    squash = jax.nn.sigmoid(gate_pre)
    return (squash, gate_pre * squash)


def body(
    tokens, labels, domain_ids, domain_weights, cotangent, gate_weight, up_weight, down_weight
):
    n_expert = lax.axis_size("expert")
    n_tensor = lax.axis_size("tensor")
    tok_rows = tokens.shape[0]
    feat_slice = tokens.shape[1]
    experts_all = n_expert // SPLIT
    capacity = SPLIT * tok_rows // experts_all
    half_cap = capacity // SPLIT
    t_idx = lax.axis_index("tensor")
    lang_label = labels[:, 0]
    dom_hot = (
        domain_ids[:, None] == jnp.arange(domain_weights.shape[0], dtype=jnp.int32)[None, :]
    ).astype(jnp.float32)
    tok_scale = jnp.sum(dom_hot * domain_weights[None, :], axis=1)
    grad_rows = (tok_scale[:, None] * cotangent.astype(jnp.float32)).astype(jnp.bfloat16)
    lab_hot = (lang_label[:, None] == jnp.arange(experts_all, dtype=jnp.int32)[None, :]).astype(
        jnp.float32
    )
    row_ids = jnp.arange(tok_rows, dtype=jnp.int32)
    earlier = (row_ids[None, :] < row_ids[:, None]).astype(jnp.float32)
    before = jnp.dot(earlier, lab_hot, preferred_element_type=jnp.float32)
    slot_pos = jnp.sum(before * lab_hot, axis=1).astype(jnp.int32)
    target_row = lang_label * capacity + slot_pos
    rows_out = n_expert * half_cap
    sources = jnp.concatenate((tokens, grad_rows), axis=1)
    dispatch_map = (
        jnp.arange(rows_out, dtype=jnp.int32)[:, None] == target_row[None, :]
    ).astype(jnp.bfloat16)
    outbound = jnp.dot(dispatch_map, sources, preferred_element_type=jnp.float32).astype(
        jnp.bfloat16
    )
    outbound = outbound.reshape(n_expert, half_cap, 2 * feat_slice)
    arrived = lax.all_to_all(outbound, "expert", split_axis=0, concat_axis=0, tiled=True)
    own_piece = arrived.reshape(rows_out, 2 * feat_slice)
    order = sorted(range(n_tensor), key=lambda k: -min(k, n_tensor - k))
    received = {k: shifted(own_piece, "tensor", k) for k in order if k}
    order = [0] + [k for k in reversed(order) if k]
    pieces = [own_piece if k == 0 else received[k] for k in order]
    blocks = []
    for p in pieces:
        both = jnp.concatenate((p, partner(p, "expert", 0)), axis=0)
        blocks.append((both[:, :feat_slice], both[:, feat_slice:]))
    src_off = [((t_idx - k) % n_tensor) * feat_slice for k in order]
    w_gate = gate_weight[0]
    w_up = up_weight[0]
    w_down = down_weight[0]
    contract_rows = (((0,), (0,)), ((), ()))
    contract_cols = (((1,), (1,)), ((), ()))

    def rows_of(w, off):
        return lax.dynamic_slice_in_dim(w, off, feat_slice, axis=0)

    def cols_of(w, off):
        return lax.dynamic_slice_in_dim(w, off, feat_slice, axis=1)

    def block_sum(terms):
        total = terms[0]
        for term in terms[1:]:
            total = total + term
        return total

    gate_pre = block_sum(
        [
            jnp.dot(b[0], rows_of(w_gate, o), preferred_element_type=jnp.float32)
            for b, o in zip(blocks, src_off)
        ]
    )
    up_pre = block_sum(
        [
            jnp.dot(b[0], rows_of(w_up, o), preferred_element_type=jnp.float32)
            for b, o in zip(blocks, src_off)
        ]
    )
    grad_hidden = block_sum(
        [
            lax.dot_general(
                b[1], cols_of(w_down, o), contract_cols, preferred_element_type=jnp.float32
            )
            for b, o in zip(blocks, src_off)
        ]
    )
    squash, activated = silu_parts(gate_pre)
    hidden = (activated * up_pre).astype(jnp.bfloat16)
    grad_gate_pre = (grad_hidden * up_pre * squash * (1.0 + gate_pre * (1.0 - squash))).astype(
        jnp.bfloat16
    )
    grad_up_pre = (grad_hidden * activated).astype(jnp.bfloat16)
    gate_grad = jnp.zeros(w_gate.shape, jnp.bfloat16)
    up_grad = jnp.zeros(w_up.shape, jnp.bfloat16)
    down_grad = jnp.zeros(w_down.shape, jnp.bfloat16)
    for b, o in zip(blocks, src_off):
        gate_piece = lax.dot_general(
            b[0], grad_gate_pre, contract_rows, preferred_element_type=jnp.float32
        ).astype(jnp.bfloat16)
        up_piece = lax.dot_general(
            b[0], grad_up_pre, contract_rows, preferred_element_type=jnp.float32
        ).astype(jnp.bfloat16)
        down_piece = lax.dot_general(
            hidden, b[1], contract_rows, preferred_element_type=jnp.float32
        ).astype(jnp.bfloat16)
        gate_grad = lax.dynamic_update_slice_in_dim(gate_grad, gate_piece, o, axis=0)
        up_grad = lax.dynamic_update_slice_in_dim(up_grad, up_piece, o, axis=0)
        down_grad = lax.dynamic_update_slice_in_dim(down_grad, down_piece, o, axis=1)
    gate_grad = gate_grad[None]
    up_grad = up_grad[None]
    down_grad = down_grad[None]
    acc = None
    for m in sorted(range(n_tensor), key=lambda k: -min(k, n_tensor - k)):
        off = ((t_idx + m) % n_tensor) * feat_slice
        out_m = jnp.dot(hidden, cols_of(w_down, off), preferred_element_type=jnp.float32)
        in_m = lax.dot_general(
            grad_gate_pre, rows_of(w_gate, off), contract_cols, preferred_element_type=jnp.float32
        ) + lax.dot_general(
            grad_up_pre, rows_of(w_up, off), contract_cols, preferred_element_type=jnp.float32
        )
        part_m = jnp.concatenate((out_m, in_m), axis=1)
        core_m = part_m[:rows_out] + partner(part_m[rows_out:], "expert", 0)
        if m:
            core_m = shifted(core_m.astype(jnp.bfloat16), "tensor", m).astype(jnp.float32)
        acc = core_m if acc is None else acc + core_m
    acc = acc.astype(jnp.bfloat16)
    going_back = jnp.stack((acc[:, :feat_slice], acc[:, feat_slice:]))
    going_back = going_back.reshape(2, n_expert, half_cap, feat_slice)
    returned = lax.all_to_all(going_back, "expert", split_axis=1, concat_axis=1, tiled=True)
    flat_back = returned.reshape(2, rows_out, feat_slice)
    home_map = (
        jnp.arange(rows_out, dtype=jnp.int32)[:, None] == target_row[None, :]
    ).astype(jnp.bfloat16)
    home = [
        lax.dot_general(
            home_map, flat_back[i], contract_rows,
            preferred_element_type=jnp.float32,
        ).astype(jnp.bfloat16)
        for i in range(2)
    ]
    return (home[0], home[1], gate_grad, up_grad, down_grad)


def solution(mesh):
    return jax.shard_map(
        body,
        mesh=mesh,
        in_specs=(
            P("expert", "tensor"),
            P("expert", None),
            P("expert"),
            P(),
            P("expert", "tensor"),
            P("expert", None, "tensor"),
            P("expert", None, "tensor"),
            P("expert", "tensor", None),
        ),
        out_specs=(
            P("expert", "tensor"),
            P("expert", "tensor"),
            P("expert", None, "tensor"),
            P("expert", None, "tensor"),
            P("expert", "tensor", None),
        ),
        check_vma=False,
    )
```

```python
import jax
import jax.numpy as jnp
from jax import lax
from jax.sharding import PartitionSpec as P

SPLIT = 2


def partner(value, axis, stride):
    return lax.ppermute(value, axis, [(i, i ^ 1 << stride) for i in range(lax.axis_size(axis))])


def shifted(value, axis, step):
    size = lax.axis_size(axis)
    return lax.ppermute(value, axis, [(i, (i + step) % size) for i in range(size)])


def silu_parts(gate_pre):
    squash = jax.nn.sigmoid(gate_pre)
    return (squash, gate_pre * squash)


def body(
    tokens, labels, domain_ids, domain_weights, cotangent, gate_weight, up_weight, down_weight
):
    n_expert = lax.axis_size("expert")
    n_tensor = lax.axis_size("tensor")
    tok_rows = tokens.shape[0]
    feat_slice = tokens.shape[1]
    experts_all = n_expert // SPLIT
    capacity = SPLIT * tok_rows // experts_all
    half_cap = capacity // SPLIT
    t_idx = lax.axis_index("tensor")
    lang_label = labels[:, 0]
    dom_hot = (
        domain_ids[:, None] == jnp.arange(domain_weights.shape[0], dtype=jnp.int32)[None, :]
    ).astype(jnp.float32)
    tok_scale = jnp.sum(dom_hot * domain_weights[None, :], axis=1)
    grad_rows = (tok_scale[:, None] * cotangent.astype(jnp.float32)).astype(jnp.bfloat16)
    row_ids = jnp.arange(tok_rows, dtype=jnp.int32)
    same_before = (lang_label[None, :] == lang_label[:, None]) & (row_ids[None, :] < row_ids[:, None])
    slot_pos = jnp.sum(same_before.astype(jnp.int32), axis=1)
    target_row = lang_label * capacity + slot_pos
    rows_out = n_expert * half_cap
    sources = jnp.concatenate((tokens, grad_rows), axis=1)
    dispatch_map = (
        jnp.arange(rows_out, dtype=jnp.int32)[:, None] == target_row[None, :]
    ).astype(jnp.bfloat16)
    outbound = jnp.dot(dispatch_map, sources, preferred_element_type=jnp.float32).astype(
        jnp.bfloat16
    )
    outbound = outbound.reshape(n_expert, half_cap, 2 * feat_slice)
    arrived = lax.all_to_all(outbound, "expert", split_axis=0, concat_axis=0, tiled=True)
    own_piece = arrived.reshape(rows_out, 2 * feat_slice)
    order = sorted(range(n_tensor), key=lambda k: -min(k, n_tensor - k))
    received = {k: shifted(own_piece, "tensor", k) for k in order if k}
    order = [0] + [k for k in reversed(order) if k]
    pieces = [own_piece if k == 0 else received[k] for k in order]
    blocks = []
    for p in pieces:
        both = jnp.concatenate((p, partner(p, "expert", 0)), axis=0)
        blocks.append((both[:, :feat_slice], both[:, feat_slice:]))
    src_off = [((t_idx - k) % n_tensor) * feat_slice for k in order]
    w_gate = gate_weight[0]
    w_up = up_weight[0]
    w_down = down_weight[0]
    contract_rows = (((0,), (0,)), ((), ()))
    contract_cols = (((1,), (1,)), ((), ()))

    def rows_of(w, off):
        return lax.dynamic_slice_in_dim(w, off, feat_slice, axis=0)

    def cols_of(w, off):
        return lax.dynamic_slice_in_dim(w, off, feat_slice, axis=1)

    def block_sum(terms):
        total = terms[0]
        for term in terms[1:]:
            total = total + term
        return total

    gate_pre = block_sum(
        [
            jnp.dot(b[0], rows_of(w_gate, o), preferred_element_type=jnp.float32)
            for b, o in zip(blocks, src_off)
        ]
    )
    up_pre = block_sum(
        [
            jnp.dot(b[0], rows_of(w_up, o), preferred_element_type=jnp.float32)
            for b, o in zip(blocks, src_off)
        ]
    )
    grad_hidden = block_sum(
        [
            lax.dot_general(
                b[1], cols_of(w_down, o), contract_cols, preferred_element_type=jnp.float32
            )
            for b, o in zip(blocks, src_off)
        ]
    )
    squash, activated = silu_parts(gate_pre)
    hidden = (activated * up_pre).astype(jnp.bfloat16)
    grad_gate_pre = (grad_hidden * up_pre * squash * (1.0 + gate_pre * (1.0 - squash))).astype(
        jnp.bfloat16
    )
    grad_up_pre = (grad_hidden * activated).astype(jnp.bfloat16)
    gate_grad = jnp.zeros(w_gate.shape, jnp.bfloat16)
    up_grad = jnp.zeros(w_up.shape, jnp.bfloat16)
    down_grad = jnp.zeros(w_down.shape, jnp.bfloat16)
    for b, o in zip(blocks, src_off):
        gate_piece = lax.dot_general(
            b[0], grad_gate_pre, contract_rows, preferred_element_type=jnp.float32
        ).astype(jnp.bfloat16)
        up_piece = lax.dot_general(
            b[0], grad_up_pre, contract_rows, preferred_element_type=jnp.float32
        ).astype(jnp.bfloat16)
        down_piece = lax.dot_general(
            hidden, b[1], contract_rows, preferred_element_type=jnp.float32
        ).astype(jnp.bfloat16)
        gate_grad = lax.dynamic_update_slice_in_dim(gate_grad, gate_piece, o, axis=0)
        up_grad = lax.dynamic_update_slice_in_dim(up_grad, up_piece, o, axis=0)
        down_grad = lax.dynamic_update_slice_in_dim(down_grad, down_piece, o, axis=1)
    gate_grad = gate_grad[None]
    up_grad = up_grad[None]
    down_grad = down_grad[None]
    acc = None
    for m in sorted(range(n_tensor), key=lambda k: -min(k, n_tensor - k)):
        off = ((t_idx + m) % n_tensor) * feat_slice
        out_m = jnp.dot(hidden, cols_of(w_down, off), preferred_element_type=jnp.float32)
        in_m = lax.dot_general(
            grad_gate_pre, rows_of(w_gate, off), contract_cols, preferred_element_type=jnp.float32
        ) + lax.dot_general(
            grad_up_pre, rows_of(w_up, off), contract_cols, preferred_element_type=jnp.float32
        )
        part_m = jnp.concatenate((out_m, in_m), axis=1)
        core_m = part_m[:rows_out] + partner(part_m[rows_out:], "expert", 0)
        if m:
            core_m = shifted(core_m.astype(jnp.bfloat16), "tensor", m).astype(jnp.float32)
        acc = core_m if acc is None else acc + core_m
    acc = acc.astype(jnp.bfloat16)
    going_back = jnp.stack((acc[:, :feat_slice], acc[:, feat_slice:]))
    going_back = going_back.reshape(2, n_expert, half_cap, feat_slice)
    returned = lax.all_to_all(going_back, "expert", split_axis=1, concat_axis=1, tiled=True)
    flat_back = returned.reshape(2, rows_out, feat_slice)
    home_map = (
        jnp.arange(rows_out, dtype=jnp.int32)[:, None] == target_row[None, :]
    ).astype(jnp.bfloat16)
    home = [
        lax.dot_general(
            home_map, flat_back[i], contract_rows,
            preferred_element_type=jnp.float32,
        ).astype(jnp.bfloat16)
        for i in range(2)
    ]
    return (home[0], home[1], gate_grad, up_grad, down_grad)


def solution(mesh):
    return jax.shard_map(
        body,
        mesh=mesh,
        in_specs=(
            P("expert", "tensor"),
            P("expert", None),
            P("expert"),
            P(),
            P("expert", "tensor"),
            P("expert", None, "tensor"),
            P("expert", None, "tensor"),
            P("expert", "tensor", None),
        ),
        out_specs=(
            P("expert", "tensor"),
            P("expert", "tensor"),
            P("expert", None, "tensor"),
            P("expert", None, "tensor"),
            P("expert", "tensor", None),
        ),
        check_vma=False,
    )
```

```python
import jax
import jax.numpy as jnp
from jax import lax
from jax.sharding import PartitionSpec as P

SPLIT = 2


def partner(value, axis, stride):
    return lax.ppermute(value, axis, [(i, i ^ 1 << stride) for i in range(lax.axis_size(axis))])


def shifted(value, axis, step):
    size = lax.axis_size(axis)
    return lax.ppermute(value, axis, [(i, (i + step) % size) for i in range(size)])


def silu_parts(gate_pre):
    squash = jax.nn.sigmoid(gate_pre)
    return (squash, gate_pre * squash)


def body(
    tokens, labels, domain_ids, domain_weights, cotangent, gate_weight, up_weight, down_weight
):
    n_expert = lax.axis_size("expert")
    n_tensor = lax.axis_size("tensor")
    tok_rows = tokens.shape[0]
    feat_slice = tokens.shape[1]
    experts_all = n_expert // SPLIT
    capacity = SPLIT * tok_rows // experts_all
    half_cap = capacity // SPLIT
    t_idx = lax.axis_index("tensor")
    lang_label = labels[:, 0]
    dom_hot = (
        domain_ids[:, None] == jnp.arange(domain_weights.shape[0], dtype=jnp.int32)[None, :]
    ).astype(jnp.float32)
    tok_scale = jnp.sum(dom_hot * domain_weights[None, :], axis=1)
    grad_rows = (tok_scale[:, None] * cotangent.astype(jnp.float32)).astype(jnp.bfloat16)
    lab_hot = (lang_label[:, None] == jnp.arange(experts_all, dtype=jnp.int32)[None, :]).astype(
        jnp.float32
    )
    row_ids = jnp.arange(tok_rows, dtype=jnp.int32)
    earlier = (row_ids[None, :] < row_ids[:, None]).astype(jnp.float32)
    before = jnp.dot(earlier, lab_hot, preferred_element_type=jnp.float32)
    slot_pos = jnp.sum(before * lab_hot, axis=1).astype(jnp.int32)
    target_row = lang_label * capacity + slot_pos
    rows_out = n_expert * half_cap
    stacked = jnp.stack((tokens, grad_rows))
    dispatch_map = (
        jnp.arange(rows_out, dtype=jnp.int32)[:, None] == target_row[None, :]
    ).astype(jnp.bfloat16)
    outbound = jnp.einsum(
        "rt,ktw->krw", dispatch_map, stacked, preferred_element_type=jnp.float32
    ).astype(jnp.bfloat16)
    outbound = outbound.reshape(2, n_expert, half_cap, feat_slice)
    arrived = lax.all_to_all(outbound, "expert", split_axis=1, concat_axis=1, tiled=True)
    arrived = arrived.reshape(2, rows_out, feat_slice)
    own_piece = jnp.concatenate((arrived[0], arrived[1]), axis=1)
    order = sorted(range(n_tensor), key=lambda k: -min(k, n_tensor - k))
    received = {k: shifted(own_piece, "tensor", k) for k in order if k}
    order = [0] + [k for k in reversed(order) if k]
    pieces = [own_piece if k == 0 else received[k] for k in order]
    blocks = []
    for p in pieces:
        both = jnp.concatenate((p, partner(p, "expert", 0)), axis=0)
        blocks.append((both[:, :feat_slice], both[:, feat_slice:]))
    src_off = [((t_idx - k) % n_tensor) * feat_slice for k in order]
    w_gate = gate_weight[0]
    w_up = up_weight[0]
    w_down = down_weight[0]
    contract_rows = (((0,), (0,)), ((), ()))
    contract_cols = (((1,), (1,)), ((), ()))

    def rows_of(w, off):
        return lax.dynamic_slice_in_dim(w, off, feat_slice, axis=0)

    def cols_of(w, off):
        return lax.dynamic_slice_in_dim(w, off, feat_slice, axis=1)

    def block_sum(terms):
        total = terms[0]
        for term in terms[1:]:
            total = total + term
        return total

    gate_pre = block_sum(
        [
            jnp.dot(b[0], rows_of(w_gate, o), preferred_element_type=jnp.float32)
            for b, o in zip(blocks, src_off)
        ]
    )
    up_pre = block_sum(
        [
            jnp.dot(b[0], rows_of(w_up, o), preferred_element_type=jnp.float32)
            for b, o in zip(blocks, src_off)
        ]
    )
    grad_hidden = block_sum(
        [
            lax.dot_general(
                b[1], cols_of(w_down, o), contract_cols, preferred_element_type=jnp.float32
            )
            for b, o in zip(blocks, src_off)
        ]
    )
    squash, activated = silu_parts(gate_pre)
    hidden = (activated * up_pre).astype(jnp.bfloat16)
    grad_gate_pre = (grad_hidden * up_pre * squash * (1.0 + gate_pre * (1.0 - squash))).astype(
        jnp.bfloat16
    )
    grad_up_pre = (grad_hidden * activated).astype(jnp.bfloat16)
    gate_grad = jnp.zeros(w_gate.shape, jnp.bfloat16)
    up_grad = jnp.zeros(w_up.shape, jnp.bfloat16)
    down_grad = jnp.zeros(w_down.shape, jnp.bfloat16)
    for b, o in zip(blocks, src_off):
        gate_piece = lax.dot_general(
            b[0], grad_gate_pre, contract_rows, preferred_element_type=jnp.float32
        ).astype(jnp.bfloat16)
        up_piece = lax.dot_general(
            b[0], grad_up_pre, contract_rows, preferred_element_type=jnp.float32
        ).astype(jnp.bfloat16)
        down_piece = lax.dot_general(
            hidden, b[1], contract_rows, preferred_element_type=jnp.float32
        ).astype(jnp.bfloat16)
        gate_grad = lax.dynamic_update_slice_in_dim(gate_grad, gate_piece, o, axis=0)
        up_grad = lax.dynamic_update_slice_in_dim(up_grad, up_piece, o, axis=0)
        down_grad = lax.dynamic_update_slice_in_dim(down_grad, down_piece, o, axis=1)
    gate_grad = gate_grad[None]
    up_grad = up_grad[None]
    down_grad = down_grad[None]
    acc = None
    for m in sorted(range(n_tensor), key=lambda k: -min(k, n_tensor - k)):
        off = ((t_idx + m) % n_tensor) * feat_slice
        out_m = jnp.dot(hidden, cols_of(w_down, off), preferred_element_type=jnp.float32)
        in_m = lax.dot_general(
            grad_gate_pre, rows_of(w_gate, off), contract_cols, preferred_element_type=jnp.float32
        ) + lax.dot_general(
            grad_up_pre, rows_of(w_up, off), contract_cols, preferred_element_type=jnp.float32
        )
        part_m = jnp.concatenate((out_m, in_m), axis=1)
        core_m = part_m[:rows_out] + partner(part_m[rows_out:], "expert", 0)
        if m:
            core_m = shifted(core_m.astype(jnp.bfloat16), "tensor", m).astype(jnp.float32)
        acc = core_m if acc is None else acc + core_m
    acc = acc.astype(jnp.bfloat16)
    going_back = jnp.stack((acc[:, :feat_slice], acc[:, feat_slice:]))
    going_back = going_back.reshape(2, n_expert, half_cap, feat_slice)
    returned = lax.all_to_all(going_back, "expert", split_axis=1, concat_axis=1, tiled=True)
    flat_back = returned.reshape(2, rows_out, feat_slice)
    home_map = (
        jnp.arange(rows_out, dtype=jnp.int32)[:, None] == target_row[None, :]
    ).astype(jnp.bfloat16)
    home = [
        lax.dot_general(
            home_map, flat_back[i], contract_rows,
            preferred_element_type=jnp.float32,
        ).astype(jnp.bfloat16)
        for i in range(2)
    ]
    return (home[0], home[1], gate_grad, up_grad, down_grad)


def solution(mesh):
    return jax.shard_map(
        body,
        mesh=mesh,
        in_specs=(
            P("expert", "tensor"),
            P("expert", None),
            P("expert"),
            P(),
            P("expert", "tensor"),
            P("expert", None, "tensor"),
            P("expert", None, "tensor"),
            P("expert", "tensor", None),
        ),
        out_specs=(
            P("expert", "tensor"),
            P("expert", "tensor"),
            P("expert", None, "tensor"),
            P("expert", None, "tensor"),
            P("expert", "tensor", None),
        ),
        check_vma=False,
    )
```
